32 devices in a mesh: groups: 2 (over y), cam: 4 (over z), tm: 2 (over x), chan: 2 (over core).
Axes of the slice: x: 2, y: 2, z: 4, core: 2. Of those that a mesh axis runs over, the one named last changes fastest.
Arguments:
- video: bfloat16 [16, 8, 16, 8, 256], P(('groups', 'cam'), 'tm', None, None, 'chan'), parts along dimension 0, may hold values from -6 to 6
- conv_weight: bfloat16 [27, 256, 256], P(None, None, 'chan'), may hold values from -0.078125 to 0.078125
- proj_weight: bfloat16 [256, 16], P('chan'), may hold values from -0.375 to 0.375
- rig_sizes: int32 [8], P('groups'), parts along dimension 0, may hold values from 1 to 3, as said below
- camera_order: int32 [16], P('groups'), parts along dimension 0, may hold values from 0 to 7, as said below
- owner_slot: int32 [8], P('groups'), parts along dimension 0, may hold values from 0 to 3, as said below
- cotangent: bfloat16 [8, 8, 16, 128], P(('groups', 'cam'), 'tm'), parts along dimension 0, may hold values from -6 to 6
Outputs:
- robot_latent: float32 [8, 8, 16, 128], P(('groups', 'cam'), 'tm'), parts along dimension 0
- grad_conv: bfloat16 [54, 256, 256], P('groups', None, 'chan'), parts along dimension 0
- grad_proj: float32 [512, 16], P(('groups', 'chan')), parts along dimension 0
- grad_video: bfloat16 [16, 8, 16, 8, 256], P(('groups', 'cam'), 'tm', None, None, 'chan'), parts along dimension 0
The draws below stay inside these ranges and needn't reach their ends.
There are 2 independent parts, one for each index of `groups`. The reference program is written for one: setup_inputs(seed, part) draws one part's arguments, and reference() takes and returns one part's arrays. A program takes and returns all parts, laid end to end along the dimension named above; an argument that names none is the same for every part. Nothing has to cross between parts.
Inputs may be any that keep to these rules, and one draw needn't show every extreme that they name: `rig_sizes`: the sizes sum to 8; the largest is exactly 3. `camera_order`: A permutation; the cameras whose places fall from rig_sizes[0] + ... + rig_sizes[r-1] to below rig_sizes[0] + ... + rig_sizes[r] belong to robot r. `owner_slot`: A permutation of the output rows.
All inputs are finite; a program needn't handle non-finite values.
Results may differ from the reference program's by a relative error of at most 0.0059.
Values may be sent and summed in bfloat16 or wider, within the bound.
No kernel may reach another device: no remote copies, remote signals or barrier semaphores. Data moves between devices by JAX's collectives and lax.ppermute only.
A program may use at most 128 MiB of HBM per device.

```python
import jax
import jax.numpy as jnp
from jax import lax

C = 256
LAT = 16
KT = 3
KS = 3
CAM_DEV = 2
HH = 16
WW = 8
CAMS = 8
ROBOTS = 4
FRAMES = 8
MOST = 3
N_CHAN = 2


def rig_tables(key):
    key_sizes = jax.random.fold_in(key, 101)
    key_extra = jax.random.fold_in(key, 102)
    key_order = jax.random.fold_in(key, 103)
    key_slots = jax.random.fold_in(key, 104)
    robots = ROBOTS
    index = jnp.arange(robots, dtype=jnp.int32)
    leftover = CAMS - MOST - (robots - 1)
    extra_rank = jax.random.permutation(key_extra, robots - 1).astype(jnp.int32)
    extra = (extra_rank < leftover).astype(jnp.int32)
    base = jnp.concatenate([jnp.array([MOST], jnp.int32), 1 + extra]).astype(jnp.int32)
    arrange = jax.random.permutation(key_sizes, robots).astype(jnp.int32)
    sizes = base[arrange].astype(jnp.int32)
    big_robot = jnp.sum(jnp.where(arrange == 0, index, 0)).astype(jnp.int32)
    starts = (jnp.cumsum(sizes) - sizes).astype(jnp.int32)
    big_start = jnp.sum(jnp.where(index == big_robot, starts, 0)).astype(jnp.int32)
    order = jax.random.permutation(key_order, CAMS).astype(jnp.int32)
    cam_index = jnp.arange(CAMS, dtype=jnp.int32)
    first_cam = jnp.sum(jnp.where(order == big_start, cam_index, 0)).astype(jnp.int32)
    target = ((first_cam // CAM_DEV + robots // 2) % robots).astype(jnp.int32)
    slots = jax.random.permutation(key_slots, robots).astype(jnp.int32)
    holder = jnp.sum(jnp.where(slots == target, index, 0)).astype(jnp.int32)
    big_old = jnp.sum(jnp.where(index == big_robot, slots, 0)).astype(jnp.int32)
    slots = jnp.where(index == holder, big_old, slots)
    slots = jnp.where(index == big_robot, target, slots).astype(jnp.int32)
    return (sizes, order, slots)


def draw_rig_sizes(key, part):
    return rig_tables(key)[0]


def draw_camera_order(key, part):
    return rig_tables(key)[1]


def draw_owner_slot(key, part):
    return rig_tables(key)[2]


def block_levels(rng, dims, cuts, smallest, largest):
    def one(dim, parts):
        draws = jax.random.uniform(jax.random.fold_in(jax.random.fold_in(rng, 6), dim), (parts,), jnp.float32, smallest / len(cuts), largest / len(cuts))
        return jnp.repeat(jnp.exp(draws), dims[dim] // parts).reshape((-1,) + (1,) * (len(dims) - dim - 1))

    loudness = one(*cuts[0])
    for cut in cuts[1:]:
        loudness = loudness * one(*cut)
    return loudness


def gaussian(key, shape, scale, most, shards=(), kind=jnp.bfloat16):
    loudness = block_levels(key, shape, shards, -0.22, 0.18) if shards else 1.0
    entries = jax.random.normal(key, shape, jnp.float32) * scale * loudness
    return jnp.minimum(jnp.maximum(entries, -most), most).astype(kind)


def setup_inputs(seed: int = 0, part: int = 0) -> dict:
    key_of = jax.random.split(jax.random.key(seed), 8)
    own_keys = jax.random.split(jax.random.fold_in(key_of[7], part), 8)
    video = gaussian(own_keys[0], (CAMS, FRAMES, HH, WW, C), 1.0, 6.0, ((0, 4), (1, 2), (4, 2)))
    conv_weight = gaussian(key_of[1], (KT * KS * KS, C, C), (KT * KS * KS * C) ** -0.5, 0.078125, ((2, 2),))
    proj_weight = gaussian(key_of[2], (C, LAT), C ** -0.5, 0.375, ((0, 2),))
    rig_sizes = draw_rig_sizes(jax.random.fold_in(jax.random.fold_in(key_of[7], part), 71), part)
    camera_order = draw_camera_order(jax.random.fold_in(jax.random.fold_in(key_of[7], part), 71), part)
    owner_slot = draw_owner_slot(jax.random.fold_in(jax.random.fold_in(key_of[7], part), 71), part)
    cotangent = gaussian(own_keys[6], (ROBOTS, FRAMES, HH, WW * LAT), 1.0, 6.0, ((0, 4), (1, 2)))
    return {"video": video, "conv_weight": conv_weight, "proj_weight": proj_weight, "rig_sizes": rig_sizes, "camera_order": camera_order, "owner_slot": owner_slot, "cotangent": cotangent}


def tap_offsets():
    return [(shift_t, shift_h, shift_w) for shift_t in range(KT) for shift_h in range(KS) for shift_w in range(KS)]


def forward_taps(extended, weight, frames, height, width):
    channels = extended.shape[-1]
    summed = jnp.zeros((extended.shape[0] * frames * height * width, weight.shape[2]), jnp.float32)
    for tap_index, (shift_t, shift_h, shift_w) in enumerate(tap_offsets()):
        window = extended[:, shift_t:shift_t + frames, shift_h:shift_h + height, shift_w:shift_w + width, :].reshape(-1, channels)
        summed = summed + jnp.dot(window, weight[tap_index], preferred_element_type=jnp.float32)
    return summed


def weight_taps(extended, grad_rows, frames, height, width):
    channels = extended.shape[-1]
    results = []
    for shift_t, shift_h, shift_w in tap_offsets():
        window = extended[:, shift_t:shift_t + frames, shift_h:shift_h + height, shift_w:shift_w + width, :].reshape(-1, channels)
        results.append(lax.dot_general(window, grad_rows, (((0,), (0,)), ((), ())), preferred_element_type=jnp.float32))
    return jnp.stack(results)


def input_taps(grad_rows, weight, batch, frames, height, width):
    channels = weight.shape[1]
    pad_half = KS // 2
    padded = jnp.zeros((batch, frames + KT - 1, height + KS - 1, width + KS - 1, channels), jnp.float32)
    for tap_index, (shift_t, shift_h, shift_w) in enumerate(tap_offsets()):
        backed = lax.dot_general(grad_rows, weight[tap_index], (((1,), (1,)), ((), ())), preferred_element_type=jnp.float32)
        padded = padded.at[:, shift_t:shift_t + frames, shift_h:shift_h + height, shift_w:shift_w + width, :].add(
            backed.reshape(batch, frames, height, width, channels))
    return padded[:, :, pad_half:pad_half + height, pad_half:pad_half + width, :]


def joining_matrix(rig_sizes, camera_order, owner_slot):
    robots = rig_sizes.shape[0]
    ends = jnp.cumsum(rig_sizes).astype(jnp.int32)
    robot_of = jnp.sum((ends[None, :] <= camera_order[:, None]).astype(jnp.int32), axis=1).astype(jnp.int32)
    member = robot_of[:, None] == jnp.arange(robots, dtype=jnp.int32)[None, :]
    slot_of = jnp.sum(jnp.where(member, owner_slot[None, :], 0), axis=1).astype(jnp.int32)
    count_of = jnp.sum(jnp.where(member, rig_sizes[None, :], 0), axis=1)
    share = 1.0 / count_of.astype(jnp.float32)
    placed = slot_of[None, :] == jnp.arange(robots, dtype=jnp.int32)[:, None]
    return jnp.where(placed, share[None, :], jnp.zeros_like(share)[None, :])


def reference(video, conv_weight, proj_weight, rig_sizes, camera_order, owner_slot, cotangent):
    cams, frames, height, width, channels = video.shape
    pad_half = KS // 2
    lat_width = proj_weight.shape[1]
    extended = jnp.pad(video, ((0, 0), (KT - 1, 0), (pad_half, pad_half), (pad_half, pad_half), (0, 0)))
    pre = forward_taps(extended, conv_weight, frames, height, width)
    sigma = jax.nn.sigmoid(pre)
    act = (pre * sigma).astype(jnp.bfloat16)
    latent = jnp.dot(act, proj_weight, preferred_element_type=jnp.float32).astype(jnp.bfloat16)
    mixing = joining_matrix(rig_sizes, camera_order, owner_slot)
    flat_latent = latent.reshape(cams, -1).astype(jnp.float32)
    robot_latent = jnp.dot(mixing, flat_latent, precision=lax.Precision.HIGHEST,
                           preferred_element_type=jnp.float32).reshape(mixing.shape[0], frames, height, width * lat_width)
    flat_cot = cotangent.reshape(mixing.shape[0], -1).astype(jnp.float32)
    dlatent = lax.dot_general(mixing, flat_cot, (((0,), (0,)), ((), ())), precision=lax.Precision.HIGHEST,
                              preferred_element_type=jnp.float32).astype(jnp.bfloat16).reshape(-1, lat_width)
    grad_proj = lax.dot_general(act, dlatent, (((0,), (0,)), ((), ())), preferred_element_type=jnp.float32)
    dact = lax.dot_general(dlatent, proj_weight, (((1,), (1,)), ((), ())), preferred_element_type=jnp.float32)
    dpre = (dact * sigma * (1.0 + pre * (1.0 - sigma))).astype(jnp.bfloat16)
    grad_conv = weight_taps(extended, dpre, frames, height, width).astype(jnp.bfloat16)
    group_width = channels // N_CHAN
    grad_video = jnp.zeros((cams, frames, height, width, channels), jnp.float32)
    for group in range(N_CHAN):
        lower = group * group_width
        part_grad = input_taps(dpre[:, lower:lower + group_width], conv_weight[:, :, lower:lower + group_width],
                               cams, frames, height, width)
        rounded = lax.optimization_barrier(part_grad[:, KT - 1:].astype(jnp.bfloat16))
        grad_video = grad_video + rounded.astype(jnp.float32)
    return robot_latent, grad_conv, grad_proj, grad_video.astype(jnp.bfloat16)
```

```python
import jax
import jax.numpy as jnp
from jax import lax
from jax.sharding import PartitionSpec as P

KT = 3
KS = 3


def shifted(shard, axis, by):
    size = lax.axis_size(axis)
    pairs = [(i, i + by) for i in range(size) if 0 <= i + by < size]
    return lax.ppermute(shard, axis, pairs)


def conv3d(lhs, rhs, padding, specs):
    return lax.conv_general_dilated(
        lhs,
        rhs,
        window_strides=(1, 1, 1),
        padding=padding,
        dimension_numbers=specs,
        preferred_element_type=jnp.float32,
    )


def joining_matrix(rig_sizes, camera_order, owner_slot):
    robots = rig_sizes.shape[0]
    ends = jnp.cumsum(rig_sizes)
    robot_of = jnp.sum((ends[None, :] <= camera_order[:, None]).astype(jnp.int32), axis=1)
    member = robot_of[:, None] == jnp.arange(robots, dtype=jnp.int32)[None, :]
    slot_of = jnp.sum(jnp.where(member, owner_slot[None, :], 0), axis=1)
    count_of = jnp.sum(jnp.where(member, rig_sizes[None, :], 0), axis=1)
    share = 1.0 / count_of.astype(jnp.float32)
    placed = slot_of[None, :] == jnp.arange(robots, dtype=jnp.int32)[:, None]
    return jnp.where(placed, share[None, :], jnp.zeros_like(share)[None, :])


def body(video, conv_weight, proj_weight, rig_sizes, camera_order, owner_slot, cotangent):
    cam_dev, frames, height, width, half_chan = video.shape
    pad_half = KS // 2
    lat_width = proj_weight.shape[1]
    out_half = conv_weight.shape[2]
    cache_half = shifted(video[:, frames - (KT - 1) :], "tm", 1)
    whole_now, whole_cache = (
        lax.all_gather(video, "chan", axis=4, tiled=True),
        lax.all_gather(cache_half, "chan", axis=4, tiled=True),
    )
    timed = jnp.concatenate([whole_cache, whole_now], axis=1)
    kernel = conv_weight.reshape(KT, KS, KS, conv_weight.shape[1], out_half)
    space_pad = [(0, 0), (pad_half, pad_half), (pad_half, pad_half)]
    pre5 = conv3d(timed, kernel, space_pad, ("NDHWC", "DHWIO", "NDHWC"))
    pre = pre5.reshape(-1, out_half)
    sigma = jax.nn.sigmoid(pre)
    act = (pre * sigma).astype(jnp.bfloat16)
    latent_part = jnp.dot(act, proj_weight, preferred_element_type=jnp.float32)
    latent = lax.psum(latent_part, "chan").astype(jnp.bfloat16)
    mixing = joining_matrix(rig_sizes, camera_order, owner_slot)
    cam_index = lax.axis_index("cam")
    my_row = lax.dynamic_slice_in_dim(mixing, cam_index, 1, 0)
    latent_maps = latent.reshape(cam_dev, frames, height, width * lat_width)
    block_in = lax.all_gather(latent_maps, "cam", axis=0, tiled=True)
    count_in = block_in.shape[0]
    flat_in = block_in.reshape(count_in, -1).astype(jnp.float32)
    added = jnp.dot(
        my_row, flat_in, precision=lax.Precision.HIGHEST, preferred_element_type=jnp.float32
    )
    robot_latent = added.reshape(1, frames, height, width * lat_width)
    my_cols = lax.dynamic_slice_in_dim(mixing, cam_index * cam_dev, cam_dev, 1)
    block_in = lax.all_gather(cotangent, "cam", axis=0, tiled=True)
    count_in = block_in.shape[0]
    flat_in = block_in.reshape(count_in, -1).astype(jnp.float32)
    spread = lax.dot_general(
        my_cols,
        flat_in,
        (((0,), (0,)), ((), ())),
        precision=lax.Precision.HIGHEST,
        preferred_element_type=jnp.float32,
    )
    dlatent = spread.astype(jnp.bfloat16).reshape(-1, lat_width)
    grad_proj_local = lax.dot_general(
        act, dlatent, (((0,), (0,)), ((), ())), preferred_element_type=jnp.float32
    )
    dact = lax.dot_general(
        dlatent, proj_weight, (((1,), (1,)), ((), ())), preferred_element_type=jnp.float32
    )
    dpre = (dact * sigma * (1.0 + pre * (1.0 - sigma))).astype(jnp.bfloat16)
    dpre5 = dpre.reshape(cam_dev, frames, height, width, out_half)
    grad_conv_local = conv3d(timed, dpre5, space_pad, ("CDHWN", "IDHWO", "DHWNC"))
    grad_conv_local = grad_conv_local.reshape(KT * KS * KS, -1, out_half)
    grad_conv_part = lax.psum_scatter(
        grad_conv_local, ("cam", "tm"), scatter_dimension=1, tiled=True
    )
    grad_proj = lax.psum(grad_proj_local, ("cam", "tm"))
    flipped = kernel[::-1, ::-1, ::-1]
    back_pad = [(KT - 1, KT - 1), (pad_half, pad_half), (pad_half, pad_half)]
    full_back = conv3d(dpre5, flipped, back_pad, ("NDHWC", "DHWOI", "NDHWC"))
    cache_part = full_back[:, : KT - 1]
    incoming = shifted(cache_part, "tm", -1)
    own_part = full_back[:, KT - 1 :]
    own_part = own_part.at[:, frames - (KT - 1) :].add(incoming)
    grad_video = lax.psum_scatter(
        own_part.astype(jnp.bfloat16), "chan", scatter_dimension=4, tiled=True
    )
    grad_conv = lax.all_gather(
        grad_conv_part.astype(jnp.bfloat16), ("cam", "tm"), axis=1, tiled=True
    )
    return (robot_latent, grad_conv, grad_proj, grad_video)


def solution(mesh):
    return jax.shard_map(
        body,
        mesh=mesh,
        in_specs=(
            P(("groups", "cam"), "tm", None, None, "chan"),
            P(None, None, "chan"),
            P("chan", None),
            P("groups"),
            P("groups"),
            P("groups"),
            P(("groups", "cam"), "tm", None, None),
        ),
        out_specs=(
            P(("groups", "cam"), "tm", None, None),
            P("groups", None, "chan"),
            P(("groups", "chan"), None),
            P(("groups", "cam"), "tm", None, None, "chan"),
        ),
        check_vma=False,
    )
```

```python
import jax
import jax.numpy as jnp
from jax import lax
from jax.sharding import PartitionSpec as P

KT = 3
KS = 3


def shifted(shard, axis, by):
    size = lax.axis_size(axis)
    pairs = [(i, i + by) for i in range(size) if 0 <= i + by < size]
    return lax.ppermute(shard, axis, pairs)


def conv3d(lhs, rhs, padding, specs):
    return lax.conv_general_dilated(
        lhs,
        rhs,
        window_strides=(1, 1, 1),
        padding=padding,
        dimension_numbers=specs,
        preferred_element_type=jnp.float32,
    )


def joining_matrix(rig_sizes, camera_order, owner_slot):
    robots = rig_sizes.shape[0]
    ends = jnp.cumsum(rig_sizes)
    robot_of = jnp.sum((ends[None, :] <= camera_order[:, None]).astype(jnp.int32), axis=1)
    member = robot_of[:, None] == jnp.arange(robots, dtype=jnp.int32)[None, :]
    slot_of = jnp.sum(jnp.where(member, owner_slot[None, :], 0), axis=1)
    count_of = jnp.sum(jnp.where(member, rig_sizes[None, :], 0), axis=1)
    share = 1.0 / count_of.astype(jnp.float32)
    placed = slot_of[None, :] == jnp.arange(robots, dtype=jnp.int32)[:, None]
    return jnp.where(placed, share[None, :], jnp.zeros_like(share)[None, :])


def body(video, conv_weight, proj_weight, rig_sizes, camera_order, owner_slot, cotangent):
    cam_dev, frames, height, width, half_chan = video.shape
    pad_half = KS // 2
    lat_width = proj_weight.shape[1]
    out_half = conv_weight.shape[2]
    cache_half = shifted(video[:, frames - (KT - 1) :], "tm", 1)
    whole_now, whole_cache = (
        lax.all_gather(video, "chan", axis=4, tiled=True),
        lax.all_gather(cache_half, "chan", axis=4, tiled=True),
    )
    timed = jnp.concatenate([whole_cache, whole_now], axis=1)
    kernel = conv_weight.reshape(KT, KS, KS, conv_weight.shape[1], out_half)
    space_pad = [(0, 0), (pad_half, pad_half), (pad_half, pad_half)]
    pre5 = conv3d(timed, kernel, space_pad, ("NDHWC", "DHWIO", "NDHWC"))
    pre = pre5.reshape(-1, out_half)
    sigma = jax.nn.sigmoid(pre)
    act = (pre * sigma).astype(jnp.bfloat16)
    latent_part = jnp.dot(act, proj_weight, preferred_element_type=jnp.float32)
    latent = lax.psum(latent_part, "chan").astype(jnp.bfloat16)
    mixing = joining_matrix(rig_sizes, camera_order, owner_slot)
    cam_index = lax.axis_index("cam")
    cam_count = lax.axis_size("cam")
    my_row = lax.dynamic_slice_in_dim(mixing, cam_index, 1, 0)
    latent_maps = latent.reshape(cam_dev, frames, height, width * lat_width)
    both = jnp.concatenate([latent_maps, cotangent], axis=0)
    both_in = lax.all_gather(both, "cam", axis=0, tiled=False)
    flat_in = both_in[:, :cam_dev].reshape(cam_count * cam_dev, -1).astype(jnp.float32)
    added = jnp.dot(
        my_row, flat_in, precision=lax.Precision.HIGHEST, preferred_element_type=jnp.float32
    )
    robot_latent = added.reshape(1, frames, height, width * lat_width)
    my_cols = lax.dynamic_slice_in_dim(mixing, cam_index * cam_dev, cam_dev, 1)
    flat_in = both_in[:, cam_dev:].reshape(cam_count * cotangent.shape[0], -1).astype(jnp.float32)
    spread = lax.dot_general(
        my_cols,
        flat_in,
        (((0,), (0,)), ((), ())),
        precision=lax.Precision.HIGHEST,
        preferred_element_type=jnp.float32,
    )
    dlatent = spread.astype(jnp.bfloat16).reshape(-1, lat_width)
    grad_proj_local = lax.dot_general(
        act, dlatent, (((0,), (0,)), ((), ())), preferred_element_type=jnp.float32
    )
    dact = lax.dot_general(
        dlatent, proj_weight, (((1,), (1,)), ((), ())), preferred_element_type=jnp.float32
    )
    dpre = (dact * sigma * (1.0 + pre * (1.0 - sigma))).astype(jnp.bfloat16)
    dpre5 = dpre.reshape(cam_dev, frames, height, width, out_half)
    grad_conv_local = conv3d(timed, dpre5, space_pad, ("CDHWN", "IDHWO", "DHWNC"))
    grad_conv_local = grad_conv_local.reshape(KT * KS * KS, -1, out_half)
    grad_conv_part = lax.psum_scatter(
        grad_conv_local, ("cam", "tm"), scatter_dimension=1, tiled=True
    )
    grad_proj = lax.psum(grad_proj_local, ("cam", "tm"))
    flipped = kernel[::-1, ::-1, ::-1]
    back_specs = ("NDHWC", "DHWOI", "NDHWC")
    head_pad = [(KT - 1, 0), (pad_half, pad_half), (pad_half, pad_half)]
    cache_part = conv3d(dpre5[:, : KT - 1], flipped, head_pad, back_specs)
    incoming = shifted(cache_part, "tm", -1)
    tail_pad = [(0, KT - 1), (pad_half, pad_half), (pad_half, pad_half)]
    own_part = conv3d(dpre5, flipped, tail_pad, back_specs)
    own_part = own_part.at[:, frames - (KT - 1) :].add(incoming)
    rounded = own_part.astype(jnp.bfloat16)
    chan_count = lax.axis_size("chan")
    chan_index = lax.axis_index("chan")
    width_out = rounded.shape[4] // chan_count
    summed = lax.dynamic_slice_in_dim(rounded, chan_index * width_out, width_out, 4).astype(
        jnp.float32
    )
    for step in range(1, chan_count):
        target = (chan_index + step) % chan_count
        sent = lax.dynamic_slice_in_dim(rounded, target * width_out, width_out, 4)
        pairs = [(i, (i + step) % chan_count) for i in range(chan_count)]
        summed = summed + lax.ppermute(sent, "chan", pairs).astype(jnp.float32)
    grad_video = summed.astype(jnp.bfloat16)
    grad_conv = lax.all_gather(
        grad_conv_part.astype(jnp.bfloat16), ("cam", "tm"), axis=1, tiled=True
    )
    return (robot_latent, grad_conv, grad_proj, grad_video)


def solution(mesh):
    return jax.shard_map(
        body,
        mesh=mesh,
        in_specs=(
            P(("groups", "cam"), "tm", None, None, "chan"),
            P(None, None, "chan"),
            P("chan", None),
            P("groups"),
            P("groups"),
            P("groups"),
            P(("groups", "cam"), "tm", None, None),
        ),
        out_specs=(
            P(("groups", "cam"), "tm", None, None),
            P("groups", None, "chan"),
            P(("groups", "chan"), None),
            P(("groups", "cam"), "tm", None, None, "chan"),
        ),
        check_vma=False,
    )
```

```python
import jax
import jax.numpy as jnp
from jax import lax
from jax.sharding import PartitionSpec as P

KT = 3
KS = 3


def shifted(shard, axis, by):
    size = lax.axis_size(axis)
    pairs = [(i, i + by) for i in range(size) if 0 <= i + by < size]
    return lax.ppermute(shard, axis, pairs)


def gathered(block, axis):
    size = lax.axis_size(axis)
    if size & (size - 1):
        return lax.all_gather(block, axis, axis=0, tiled=True)
    index = lax.axis_index(axis)
    blocks = block
    step = 1
    while step < size:
        pairs = [(i, i ^ step) for i in range(size)]
        other = lax.ppermute(blocks, axis, pairs)
        upper = (index & step) != 0
        blocks = jnp.where(
            upper,
            jnp.concatenate([other, blocks], axis=0),
            jnp.concatenate([blocks, other], axis=0),
        )
        step *= 2
    return blocks


def conv3d(lhs, rhs, padding, specs):
    return lax.conv_general_dilated(
        lhs,
        rhs,
        window_strides=(1, 1, 1),
        padding=padding,
        dimension_numbers=specs,
        preferred_element_type=jnp.float32,
    )


def joining_matrix(rig_sizes, camera_order, owner_slot):
    robots = rig_sizes.shape[0]
    ends = jnp.cumsum(rig_sizes)
    robot_of = jnp.sum((ends[None, :] <= camera_order[:, None]).astype(jnp.int32), axis=1)
    member = robot_of[:, None] == jnp.arange(robots, dtype=jnp.int32)[None, :]
    slot_of = jnp.sum(jnp.where(member, owner_slot[None, :], 0), axis=1)
    count_of = jnp.sum(jnp.where(member, rig_sizes[None, :], 0), axis=1)
    share = 1.0 / count_of.astype(jnp.float32)
    placed = slot_of[None, :] == jnp.arange(robots, dtype=jnp.int32)[:, None]
    return jnp.where(placed, share[None, :], jnp.zeros_like(share)[None, :])


def body(video, conv_weight, proj_weight, rig_sizes, camera_order, owner_slot, cotangent):
    cam_dev, frames, height, width, half_chan = video.shape
    pad_half = KS // 2
    lat_width = proj_weight.shape[1]
    out_half = conv_weight.shape[2]
    cache_half = shifted(video[:, frames - (KT - 1) :], "tm", 1)
    whole_now, whole_cache = (
        lax.all_gather(video, "chan", axis=4, tiled=True),
        lax.all_gather(cache_half, "chan", axis=4, tiled=True),
    )
    timed = jnp.concatenate([whole_cache, whole_now], axis=1)
    kernel = conv_weight.reshape(KT, KS, KS, conv_weight.shape[1], out_half)
    space_pad = [(0, 0), (pad_half, pad_half), (pad_half, pad_half)]
    pre5 = conv3d(timed, kernel, space_pad, ("NDHWC", "DHWIO", "NDHWC"))
    pre = pre5.reshape(-1, out_half)
    sigma = jax.nn.sigmoid(pre)
    act = (pre * sigma).astype(jnp.bfloat16)
    latent_part = jnp.dot(act, proj_weight, preferred_element_type=jnp.float32)
    latent = lax.psum(latent_part, "chan").astype(jnp.bfloat16)
    mixing = joining_matrix(rig_sizes, camera_order, owner_slot)
    cam_index = lax.axis_index("cam")
    my_row = lax.dynamic_slice_in_dim(mixing, cam_index, 1, 0)
    latent_maps = latent.reshape(cam_dev, frames, height, width * lat_width)
    block_in = gathered(latent_maps, "cam")
    flat_in = block_in.reshape(block_in.shape[0], -1).astype(jnp.float32)
    added = jnp.dot(
        my_row, flat_in, precision=lax.Precision.HIGHEST, preferred_element_type=jnp.float32
    )
    robot_latent = added.reshape(1, frames, height, width * lat_width)
    my_cols = lax.dynamic_slice_in_dim(mixing, cam_index * cam_dev, cam_dev, 1)
    block_in = gathered(cotangent, "cam")
    flat_in = block_in.reshape(block_in.shape[0], -1).astype(jnp.float32)
    spread = lax.dot_general(
        my_cols,
        flat_in,
        (((0,), (0,)), ((), ())),
        precision=lax.Precision.HIGHEST,
        preferred_element_type=jnp.float32,
    )
    dlatent = spread.astype(jnp.bfloat16).reshape(-1, lat_width)
    grad_proj_local = lax.dot_general(
        act, dlatent, (((0,), (0,)), ((), ())), preferred_element_type=jnp.float32
    )
    dact = lax.dot_general(
        dlatent, proj_weight, (((1,), (1,)), ((), ())), preferred_element_type=jnp.float32
    )
    dpre = (dact * sigma * (1.0 + pre * (1.0 - sigma))).astype(jnp.bfloat16)
    dpre5 = dpre.reshape(cam_dev, frames, height, width, out_half)
    grad_conv_local = conv3d(timed, dpre5, space_pad, ("CDHWN", "IDHWO", "DHWNC"))
    grad_conv_local = grad_conv_local.reshape(KT * KS * KS, -1, out_half)
    grad_conv_part = lax.psum_scatter(
        grad_conv_local.astype(jnp.bfloat16), ("cam", "tm"), scatter_dimension=1, tiled=True
    )
    grad_proj = lax.psum(grad_proj_local, ("cam", "tm"))
    flipped = kernel[::-1, ::-1, ::-1]
    back_specs = ("NDHWC", "DHWOI", "NDHWC")
    head_pad = [(KT - 1, 0), (pad_half, pad_half), (pad_half, pad_half)]
    cache_part = conv3d(dpre5[:, : KT - 1], flipped, head_pad, back_specs)
    incoming = shifted(cache_part, "tm", -1)
    tail_pad = [(0, KT - 1), (pad_half, pad_half), (pad_half, pad_half)]
    own_part = conv3d(dpre5, flipped, tail_pad, back_specs)
    own_part = own_part.at[:, frames - (KT - 1) :].add(incoming)
    rounded = own_part.astype(jnp.bfloat16)
    chan_count = lax.axis_size("chan")
    chan_index = lax.axis_index("chan")
    width_out = rounded.shape[4] // chan_count
    summed = lax.dynamic_slice_in_dim(rounded, chan_index * width_out, width_out, 4).astype(
        jnp.float32
    )
    for step in range(1, chan_count):
        target = (chan_index + step) % chan_count
        sent = lax.dynamic_slice_in_dim(rounded, target * width_out, width_out, 4)
        pairs = [(i, (i + step) % chan_count) for i in range(chan_count)]
        summed = summed + lax.ppermute(sent, "chan", pairs).astype(jnp.float32)
    grad_video = summed.astype(jnp.bfloat16)
    grad_conv = lax.all_gather(
        grad_conv_part.astype(jnp.bfloat16), ("cam", "tm"), axis=1, tiled=True
    )
    return (robot_latent, grad_conv, grad_proj, grad_video)


def solution(mesh):
    return jax.shard_map(
        body,
        mesh=mesh,
        in_specs=(
            P(("groups", "cam"), "tm", None, None, "chan"),
            P(None, None, "chan"),
            P("chan", None),
            P("groups"),
            P("groups"),
            P("groups"),
            P(("groups", "cam"), "tm", None, None),
        ),
        out_specs=(
            P(("groups", "cam"), "tm", None, None),
            P("groups", None, "chan"),
            P(("groups", "chan"), None),
            P(("groups", "cam"), "tm", None, None, "chan"),
        ),
        check_vma=False,
    )
```

```python
import jax
import jax.numpy as jnp
from jax import lax
from jax.sharding import PartitionSpec as P

KT = 3
KS = 3


def shifted(shard, axis, by):
    size = lax.axis_size(axis)
    pairs = [(i, i + by) for i in range(size) if 0 <= i + by < size]
    return lax.ppermute(shard, axis, pairs)


def group_place(axes):
    count = 1
    index = 0
    for axis in axes:
        count *= lax.axis_size(axis)
        index = index * lax.axis_size(axis) + lax.axis_index(axis)
    return count, index


def from_all(block, axes, count):
    received = [block]
    for step in range(1, count):
        pairs = [(i, (i - step) % count) for i in range(count)]
        received.append(lax.ppermute(block, axes, pairs))
    return jnp.stack(received, 0)


def rows_scatter_sum(rows, axes):
    count, index = group_place(axes)
    if count > 8:
        return lax.psum_scatter(rows, axes, scatter_dimension=0, tiled=True)
    piece = rows.shape[0] // count
    summed = lax.dynamic_slice_in_dim(rows, index * piece, piece, 0)
    for step in range(1, count):
        target = (index + step) % count
        part = lax.dynamic_slice_in_dim(rows, target * piece, piece, 0)
        pairs = [(i, (i + step) % count) for i in range(count)]
        summed = summed + lax.ppermute(part, axes, pairs)
    return summed


def rows_gather(rows, axes):
    count, index = group_place(axes)
    if count > 8:
        return lax.all_gather(rows, axes, axis=0, tiled=True)
    stacked = jnp.roll(from_all(rows, axes, count), index, axis=0)
    return stacked.reshape(count * rows.shape[0], *rows.shape[1:])


def ordered_sum(block, axes):
    count, index = group_place(axes)
    if count > 8:
        return lax.psum(block, axes)
    stacked = jnp.roll(from_all(block, axes, count), index, axis=0)
    return jnp.sum(stacked, axis=0)


def gathered(block, axis):
    size = lax.axis_size(axis)
    if size & (size - 1):
        return lax.all_gather(block, axis, axis=0, tiled=True)
    index = lax.axis_index(axis)
    blocks = block
    step = 1
    while step < size:
        pairs = [(i, i ^ step) for i in range(size)]
        other = lax.ppermute(blocks, axis, pairs)
        upper = (index & step) != 0
        blocks = jnp.where(
            upper,
            jnp.concatenate([other, blocks], axis=0),
            jnp.concatenate([blocks, other], axis=0),
        )
        step *= 2
    return blocks


def conv3d(lhs, rhs, padding, specs):
    return lax.conv_general_dilated(
        lhs,
        rhs,
        window_strides=(1, 1, 1),
        padding=padding,
        dimension_numbers=specs,
        preferred_element_type=jnp.float32,
    )


def joining_matrix(rig_sizes, camera_order, owner_slot):
    robots = rig_sizes.shape[0]
    ends = jnp.cumsum(rig_sizes)
    robot_of = jnp.sum((ends[None, :] <= camera_order[:, None]).astype(jnp.int32), axis=1)
    member = robot_of[:, None] == jnp.arange(robots, dtype=jnp.int32)[None, :]
    slot_of = jnp.sum(jnp.where(member, owner_slot[None, :], 0), axis=1)
    count_of = jnp.sum(jnp.where(member, rig_sizes[None, :], 0), axis=1)
    share = 1.0 / count_of.astype(jnp.float32)
    placed = slot_of[None, :] == jnp.arange(robots, dtype=jnp.int32)[:, None]
    return jnp.where(placed, share[None, :], jnp.zeros_like(share)[None, :])


def body(video, conv_weight, proj_weight, rig_sizes, camera_order, owner_slot, cotangent):
    cam_dev, frames, height, width, half_chan = video.shape
    pad_half = KS // 2
    lat_width = proj_weight.shape[1]
    out_half = conv_weight.shape[2]
    cache_half = shifted(video[:, frames - (KT - 1) :], "tm", 1)
    whole_now, whole_cache = (
        lax.all_gather(video, "chan", axis=4, tiled=True),
        lax.all_gather(cache_half, "chan", axis=4, tiled=True),
    )
    timed = jnp.concatenate([whole_cache, whole_now], axis=1)
    kernel = conv_weight.reshape(KT, KS, KS, conv_weight.shape[1], out_half)
    space_pad = [(0, 0), (pad_half, pad_half), (pad_half, pad_half)]
    pre5 = conv3d(timed, kernel, space_pad, ("NDHWC", "DHWIO", "NDHWC"))
    pre = pre5.reshape(-1, out_half)
    sigma = jax.nn.sigmoid(pre)
    act = (pre * sigma).astype(jnp.bfloat16)
    latent_part = jnp.dot(act, proj_weight, preferred_element_type=jnp.float32)
    latent = lax.psum(latent_part, "chan").astype(jnp.bfloat16)
    mixing = joining_matrix(rig_sizes, camera_order, owner_slot)
    cam_index = lax.axis_index("cam")
    my_row = lax.dynamic_slice_in_dim(mixing, cam_index, 1, 0)
    latent_maps = latent.reshape(cam_dev, frames, height, width * lat_width)
    block_in = gathered(latent_maps, "cam")
    flat_in = block_in.reshape(block_in.shape[0], -1).astype(jnp.float32)
    added = jnp.dot(
        my_row, flat_in, precision=lax.Precision.HIGHEST, preferred_element_type=jnp.float32
    )
    robot_latent = added.reshape(1, frames, height, width * lat_width)
    my_cols = lax.dynamic_slice_in_dim(mixing, cam_index * cam_dev, cam_dev, 1)
    block_in = gathered(cotangent, "cam")
    flat_in = block_in.reshape(block_in.shape[0], -1).astype(jnp.float32)
    spread = lax.dot_general(
        my_cols,
        flat_in,
        (((0,), (0,)), ((), ())),
        precision=lax.Precision.HIGHEST,
        preferred_element_type=jnp.float32,
    )
    dlatent = spread.astype(jnp.bfloat16).reshape(-1, lat_width)
    grad_proj_local = lax.dot_general(
        act, dlatent, (((0,), (0,)), ((), ())), preferred_element_type=jnp.float32
    )
    dact = lax.dot_general(
        dlatent, proj_weight, (((1,), (1,)), ((), ())), preferred_element_type=jnp.float32
    )
    dpre = (dact * sigma * (1.0 + pre * (1.0 - sigma))).astype(jnp.bfloat16)
    dpre5 = dpre.reshape(cam_dev, frames, height, width, out_half)
    grad_conv_local = conv3d(timed, dpre5, space_pad, ("CDHWN", "IDHWO", "DHWNC"))
    grad_conv_rows = grad_conv_local.reshape(-1, out_half)
    grad_conv_part = rows_scatter_sum(grad_conv_rows, ("cam", "tm"))
    grad_proj = ordered_sum(grad_proj_local, ("cam", "tm"))
    flipped = kernel[::-1, ::-1, ::-1]
    back_specs = ("NDHWC", "DHWOI", "NDHWC")
    head_pad = [(KT - 1, 0), (pad_half, pad_half), (pad_half, pad_half)]
    cache_part = conv3d(dpre5[:, : KT - 1], flipped, head_pad, back_specs)
    incoming = shifted(cache_part, "tm", -1)
    tail_pad = [(0, KT - 1), (pad_half, pad_half), (pad_half, pad_half)]
    own_part = conv3d(dpre5, flipped, tail_pad, back_specs)
    own_part = own_part.at[:, frames - (KT - 1) :].add(incoming)
    rounded = own_part.astype(jnp.bfloat16)
    chan_count = lax.axis_size("chan")
    chan_index = lax.axis_index("chan")
    width_out = rounded.shape[4] // chan_count
    summed = lax.dynamic_slice_in_dim(rounded, chan_index * width_out, width_out, 4).astype(
        jnp.float32
    )
    for step in range(1, chan_count):
        target = (chan_index + step) % chan_count
        sent = lax.dynamic_slice_in_dim(rounded, target * width_out, width_out, 4)
        pairs = [(i, (i + step) % chan_count) for i in range(chan_count)]
        summed = summed + lax.ppermute(sent, "chan", pairs).astype(jnp.float32)
    grad_video = summed.astype(jnp.bfloat16)
    grad_conv = rows_gather(grad_conv_part.astype(jnp.bfloat16), ("cam", "tm")).reshape(
        KT * KS * KS, -1, out_half
    )
    return (robot_latent, grad_conv, grad_proj, grad_video)


def solution(mesh):
    return jax.shard_map(
        body,
        mesh=mesh,
        in_specs=(
            P(("groups", "cam"), "tm", None, None, "chan"),
            P(None, None, "chan"),
            P("chan", None),
            P("groups"),
            P("groups"),
            P("groups"),
            P(("groups", "cam"), "tm", None, None),
        ),
        out_specs=(
            P(("groups", "cam"), "tm", None, None),
            P("groups", None, "chan"),
            P(("groups", "chan"), None),
            P(("groups", "cam"), "tm", None, None, "chan"),
        ),
        check_vma=False,
    )
```

```python
import jax
import jax.numpy as jnp
from jax import lax
from jax.sharding import PartitionSpec as P

KT = 3
KS = 3


def shifted(shard, axis, by):
    size = lax.axis_size(axis)
    pairs = [(i, i + by) for i in range(size) if 0 <= i + by < size]
    return lax.ppermute(shard, axis, pairs)


def gathered(block, axis):
    size = lax.axis_size(axis)
    if size & (size - 1):
        return lax.all_gather(block, axis, axis=0, tiled=True)
    index = lax.axis_index(axis)
    blocks = block
    step = 1
    while step < size:
        pairs = [(i, i ^ step) for i in range(size)]
        other = lax.ppermute(blocks, axis, pairs)
        upper = (index & step) != 0
        blocks = jnp.where(
            upper,
            jnp.concatenate([other, blocks], axis=0),
            jnp.concatenate([blocks, other], axis=0),
        )
        step *= 2
    return blocks


def conv3d(lhs, rhs, padding, specs):
    return lax.conv_general_dilated(
        lhs,
        rhs,
        window_strides=(1, 1, 1),
        padding=padding,
        dimension_numbers=specs,
        preferred_element_type=jnp.float32,
    )


def joining_matrix(rig_sizes, camera_order, owner_slot):
    robots = rig_sizes.shape[0]
    ends = jnp.cumsum(rig_sizes)
    robot_of = jnp.sum((ends[None, :] <= camera_order[:, None]).astype(jnp.int32), axis=1)
    member = robot_of[:, None] == jnp.arange(robots, dtype=jnp.int32)[None, :]
    slot_of = jnp.sum(jnp.where(member, owner_slot[None, :], 0), axis=1)
    count_of = jnp.sum(jnp.where(member, rig_sizes[None, :], 0), axis=1)
    share = 1.0 / count_of.astype(jnp.float32)
    placed = slot_of[None, :] == jnp.arange(robots, dtype=jnp.int32)[:, None]
    return jnp.where(placed, share[None, :], jnp.zeros_like(share)[None, :])


def body(video, conv_weight, proj_weight, rig_sizes, camera_order, owner_slot, cotangent):
    cam_dev, frames, height, width, half_chan = video.shape
    pad_half = KS // 2
    lat_width = proj_weight.shape[1]
    out_half = conv_weight.shape[2]
    whole_now = lax.all_gather(video, "chan", axis=4, tiled=True)
    whole_cache = shifted(whole_now[:, frames - (KT - 1) :], "tm", 1)
    timed = jnp.concatenate([whole_cache, whole_now], axis=1)
    kernel = conv_weight.reshape(KT, KS, KS, conv_weight.shape[1], out_half)
    space_pad = [(0, 0), (pad_half, pad_half), (pad_half, pad_half)]
    pre5 = conv3d(timed, kernel, space_pad, ("NDHWC", "DHWIO", "NDHWC"))
    pre = pre5.reshape(-1, out_half)
    sigma = jax.nn.sigmoid(pre)
    act = (pre * sigma).astype(jnp.bfloat16)
    latent_part = jnp.dot(act, proj_weight, preferred_element_type=jnp.float32)
    latent = lax.psum(latent_part, "chan").astype(jnp.bfloat16)
    mixing = joining_matrix(rig_sizes, camera_order, owner_slot)
    cam_index = lax.axis_index("cam")
    my_row = lax.dynamic_slice_in_dim(mixing, cam_index, 1, 0)
    latent_maps = latent.reshape(cam_dev, frames, height, width * lat_width)
    block_in = gathered(latent_maps, "cam")
    flat_in = block_in.reshape(block_in.shape[0], -1).astype(jnp.float32)
    added = jnp.dot(
        my_row, flat_in, precision=lax.Precision.HIGHEST, preferred_element_type=jnp.float32
    )
    robot_latent = added.reshape(1, frames, height, width * lat_width)
    my_cols = lax.dynamic_slice_in_dim(mixing, cam_index * cam_dev, cam_dev, 1)
    block_in = gathered(cotangent, "cam")
    flat_in = block_in.reshape(block_in.shape[0], -1).astype(jnp.float32)
    spread = lax.dot_general(
        my_cols,
        flat_in,
        (((0,), (0,)), ((), ())),
        precision=lax.Precision.HIGHEST,
        preferred_element_type=jnp.float32,
    )
    dlatent = spread.astype(jnp.bfloat16).reshape(-1, lat_width)
    grad_proj_local = lax.dot_general(
        act, dlatent, (((0,), (0,)), ((), ())), preferred_element_type=jnp.float32
    )
    dact = lax.dot_general(
        dlatent, proj_weight, (((1,), (1,)), ((), ())), preferred_element_type=jnp.float32
    )
    dpre = (dact * sigma * (1.0 + pre * (1.0 - sigma))).astype(jnp.bfloat16)
    dpre5 = dpre.reshape(cam_dev, frames, height, width, out_half)
    grad_conv_local = conv3d(timed, dpre5, space_pad, ("CDHWN", "IDHWO", "DHWNC"))
    grad_conv_local = grad_conv_local.reshape(KT * KS * KS, -1, out_half)
    grad_conv_part = lax.psum_scatter(
        grad_conv_local, ("cam", "tm"), scatter_dimension=1, tiled=True
    )
    grad_proj = lax.psum(grad_proj_local, ("cam", "tm"))
    flipped = kernel[::-1, ::-1, ::-1]
    back_specs = ("NDHWC", "DHWOI", "NDHWC")
    head_pad = [(KT - 1, 0), (pad_half, pad_half), (pad_half, pad_half)]
    cache_part = conv3d(dpre5[:, : KT - 1], flipped, head_pad, back_specs)
    incoming = shifted(cache_part, "tm", -1)
    tail_pad = [(0, KT - 1), (pad_half, pad_half), (pad_half, pad_half)]
    own_part = conv3d(dpre5, flipped, tail_pad, back_specs)
    own_part = own_part.at[:, frames - (KT - 1) :].add(incoming)
    rounded = own_part.astype(jnp.bfloat16)
    chan_count = lax.axis_size("chan")
    chan_index = lax.axis_index("chan")
    width_out = rounded.shape[4] // chan_count
    summed = lax.dynamic_slice_in_dim(rounded, chan_index * width_out, width_out, 4).astype(
        jnp.float32
    )
    for step in range(1, chan_count):
        target = (chan_index + step) % chan_count
        sent = lax.dynamic_slice_in_dim(rounded, target * width_out, width_out, 4)
        pairs = [(i, (i + step) % chan_count) for i in range(chan_count)]
        summed = summed + lax.ppermute(sent, "chan", pairs).astype(jnp.float32)
    grad_video = summed.astype(jnp.bfloat16)
    grad_conv = lax.all_gather(
        grad_conv_part.astype(jnp.bfloat16), ("cam", "tm"), axis=1, tiled=True
    )
    return (robot_latent, grad_conv, grad_proj, grad_video)


def solution(mesh):
    return jax.shard_map(
        body,
        mesh=mesh,
        in_specs=(
            P(("groups", "cam"), "tm", None, None, "chan"),
            P(None, None, "chan"),
            P("chan", None),
            P("groups"),
            P("groups"),
            P("groups"),
            P(("groups", "cam"), "tm", None, None),
        ),
        out_specs=(
            P(("groups", "cam"), "tm", None, None),
            P("groups", None, "chan"),
            P(("groups", "chan"), None),
            P(("groups", "cam"), "tm", None, None, "chan"),
        ),
        check_vma=False,
    )
```

```python
import jax
import jax.numpy as jnp
from jax import lax
from jax.sharding import PartitionSpec as P

KT = 3
KS = 3


def shifted(shard, axis, by):
    size = lax.axis_size(axis)
    pairs = [(i, i + by) for i in range(size) if 0 <= i + by < size]
    return lax.ppermute(shard, axis, pairs)


def gathered(block, axis):
    size = lax.axis_size(axis)
    if size & (size - 1):
        return lax.all_gather(block, axis, axis=0, tiled=True)
    index = lax.axis_index(axis)
    blocks = block
    step = 1
    while step < size:
        pairs = [(i, i ^ step) for i in range(size)]
        other = lax.ppermute(blocks, axis, pairs)
        upper = (index & step) != 0
        blocks = jnp.where(
            upper,
            jnp.concatenate([other, blocks], axis=0),
            jnp.concatenate([blocks, other], axis=0),
        )
        step *= 2
    return blocks


def conv3d(lhs, rhs, padding, specs):
    return lax.conv_general_dilated(
        lhs,
        rhs,
        window_strides=(1, 1, 1),
        padding=padding,
        dimension_numbers=specs,
        preferred_element_type=jnp.float32,
    )


def weight_grad_sliced(whole_now, dpre5, space_pad):
    axes = ("cam", "tm")
    cams = lax.axis_size("cam")
    times = lax.axis_size("tm")
    count = cams * times
    cam_dev, frames, height, width, chans = whole_now.shape
    piece = chans // count
    chunks = whole_now.reshape(cam_dev, frames, height, width, count, piece)
    chunks = jnp.moveaxis(chunks, 4, 0)
    mine = lax.all_to_all(chunks, axes, 0, 0, tiled=True)
    mine = mine.reshape(cams, times, cam_dev, frames, height, width, piece)
    tail = mine[:, : times - 1, :, frames - (KT - 1) :]
    head = jnp.zeros((cams, 1) + tail.shape[2:], mine.dtype)
    before = jnp.concatenate([head, tail], axis=1)
    timed_all = jnp.concatenate([before, mine], axis=3)
    timed_all = timed_all.reshape(count * cam_dev, frames + KT - 1, height, width, piece)
    dpre_all = lax.all_gather(dpre5, axes, axis=0, tiled=True)
    part = conv3d(timed_all, dpre_all, space_pad, ("CDHWN", "IDHWO", "DHWNC"))
    part = part.astype(jnp.bfloat16)
    return lax.all_gather(part, axes, axis=3, tiled=True)


def joining_matrix(rig_sizes, camera_order, owner_slot):
    robots = rig_sizes.shape[0]
    ends = jnp.cumsum(rig_sizes)
    robot_of = jnp.sum((ends[None, :] <= camera_order[:, None]).astype(jnp.int32), axis=1)
    member = robot_of[:, None] == jnp.arange(robots, dtype=jnp.int32)[None, :]
    slot_of = jnp.sum(jnp.where(member, owner_slot[None, :], 0), axis=1)
    count_of = jnp.sum(jnp.where(member, rig_sizes[None, :], 0), axis=1)
    share = 1.0 / count_of.astype(jnp.float32)
    placed = slot_of[None, :] == jnp.arange(robots, dtype=jnp.int32)[:, None]
    return jnp.where(placed, share[None, :], jnp.zeros_like(share)[None, :])


def body(video, conv_weight, proj_weight, rig_sizes, camera_order, owner_slot, cotangent):
    cam_dev, frames, height, width, half_chan = video.shape
    pad_half = KS // 2
    lat_width = proj_weight.shape[1]
    out_half = conv_weight.shape[2]
    whole_now = lax.all_gather(video, "chan", axis=4, tiled=True)
    whole_cache = shifted(whole_now[:, frames - (KT - 1) :], "tm", 1)
    timed = jnp.concatenate([whole_cache, whole_now], axis=1)
    kernel = conv_weight.reshape(KT, KS, KS, conv_weight.shape[1], out_half)
    space_pad = [(0, 0), (pad_half, pad_half), (pad_half, pad_half)]
    pre5 = conv3d(timed, kernel, space_pad, ("NDHWC", "DHWIO", "NDHWC"))
    pre = pre5.reshape(-1, out_half)
    sigma = jax.nn.sigmoid(pre)
    act = (pre * sigma).astype(jnp.bfloat16)
    latent_part = jnp.dot(act, proj_weight, preferred_element_type=jnp.float32)
    latent = lax.psum(latent_part, "chan").astype(jnp.bfloat16)
    mixing = joining_matrix(rig_sizes, camera_order, owner_slot)
    cam_index = lax.axis_index("cam")
    my_row = lax.dynamic_slice_in_dim(mixing, cam_index, 1, 0)
    latent_maps = latent.reshape(cam_dev, frames, height, width * lat_width)
    block_in = gathered(latent_maps, "cam")
    flat_in = block_in.reshape(block_in.shape[0], -1).astype(jnp.float32)
    added = jnp.dot(
        my_row, flat_in, precision=lax.Precision.HIGHEST, preferred_element_type=jnp.float32
    )
    robot_latent = added.reshape(1, frames, height, width * lat_width)
    my_cols = lax.dynamic_slice_in_dim(mixing, cam_index * cam_dev, cam_dev, 1)
    block_in = gathered(cotangent, "cam")
    flat_in = block_in.reshape(block_in.shape[0], -1).astype(jnp.float32)
    spread = lax.dot_general(
        my_cols,
        flat_in,
        (((0,), (0,)), ((), ())),
        precision=lax.Precision.HIGHEST,
        preferred_element_type=jnp.float32,
    )
    dlatent = spread.astype(jnp.bfloat16).reshape(-1, lat_width)
    grad_proj_local = lax.dot_general(
        act, dlatent, (((0,), (0,)), ((), ())), preferred_element_type=jnp.float32
    )
    dact = lax.dot_general(
        dlatent, proj_weight, (((1,), (1,)), ((), ())), preferred_element_type=jnp.float32
    )
    dpre = (dact * sigma * (1.0 + pre * (1.0 - sigma))).astype(jnp.bfloat16)
    dpre5 = dpre.reshape(cam_dev, frames, height, width, out_half)
    if lax.axis_size("cam") * lax.axis_size("tm") <= 8:
        grad_conv = weight_grad_sliced(whole_now, dpre5, space_pad).reshape(
            KT * KS * KS, -1, out_half
        )
    else:
        grad_conv_local = conv3d(timed, dpre5, space_pad, ("CDHWN", "IDHWO", "DHWNC"))
        grad_conv_local = grad_conv_local.reshape(KT * KS * KS, -1, out_half)
        grad_conv_part = lax.psum_scatter(
            grad_conv_local, ("cam", "tm"), scatter_dimension=1, tiled=True
        )
        grad_conv = lax.all_gather(
            grad_conv_part.astype(jnp.bfloat16), ("cam", "tm"), axis=1, tiled=True
        )
    grad_proj = lax.psum(grad_proj_local, ("cam", "tm"))
    flipped = kernel[::-1, ::-1, ::-1]
    back_specs = ("NDHWC", "DHWOI", "NDHWC")
    head_pad = [(KT - 1, 0), (pad_half, pad_half), (pad_half, pad_half)]
    cache_part = conv3d(dpre5[:, : KT - 1], flipped, head_pad, back_specs)
    incoming = shifted(cache_part, "tm", -1)
    tail_pad = [(0, KT - 1), (pad_half, pad_half), (pad_half, pad_half)]
    own_part = conv3d(dpre5, flipped, tail_pad, back_specs)
    own_part = own_part.at[:, frames - (KT - 1) :].add(incoming)
    rounded = own_part.astype(jnp.bfloat16)
    chan_count = lax.axis_size("chan")
    chan_index = lax.axis_index("chan")
    width_out = rounded.shape[4] // chan_count
    summed = lax.dynamic_slice_in_dim(rounded, chan_index * width_out, width_out, 4).astype(
        jnp.float32
    )
    for step in range(1, chan_count):
        target = (chan_index + step) % chan_count
        sent = lax.dynamic_slice_in_dim(rounded, target * width_out, width_out, 4)
        pairs = [(i, (i + step) % chan_count) for i in range(chan_count)]
        summed = summed + lax.ppermute(sent, "chan", pairs).astype(jnp.float32)
    grad_video = summed.astype(jnp.bfloat16)
    return (robot_latent, grad_conv, grad_proj, grad_video)


def solution(mesh):
    return jax.shard_map(
        body,
        mesh=mesh,
        in_specs=(
            P(("groups", "cam"), "tm", None, None, "chan"),
            P(None, None, "chan"),
            P("chan", None),
            P("groups"),
            P("groups"),
            P("groups"),
            P(("groups", "cam"), "tm", None, None),
        ),
        out_specs=(
            P(("groups", "cam"), "tm", None, None),
            P("groups", None, "chan"),
            P(("groups", "chan"), None),
            P(("groups", "cam"), "tm", None, None, "chan"),
        ),
        check_vma=False,
    )
```

```python
import jax
import jax.numpy as jnp
from jax import lax
from jax.sharding import PartitionSpec as P

KT = 3
KS = 3


def shifted(shard, axis, by):
    size = lax.axis_size(axis)
    pairs = [(i, i + by) for i in range(size) if 0 <= i + by < size]
    return lax.ppermute(shard, axis, pairs)


def gathered(block, axis):
    size = lax.axis_size(axis)
    if size & (size - 1):
        return lax.all_gather(block, axis, axis=0, tiled=True)
    index = lax.axis_index(axis)
    blocks = block
    step = 1
    while step < size:
        pairs = [(i, i ^ step) for i in range(size)]
        other = lax.ppermute(blocks, axis, pairs)
        upper = (index & step) != 0
        blocks = jnp.where(
            upper,
            jnp.concatenate([other, blocks], axis=0),
            jnp.concatenate([blocks, other], axis=0),
        )
        step *= 2
    return blocks


def conv3d(lhs, rhs, padding, specs):
    return lax.conv_general_dilated(
        lhs,
        rhs,
        window_strides=(1, 1, 1),
        padding=padding,
        dimension_numbers=specs,
        preferred_element_type=jnp.float32,
    )


def weight_grad_sliced(whole_now, dpre5, space_pad):
    axes = ("cam", "tm")
    cams = lax.axis_size("cam")
    times = lax.axis_size("tm")
    count = cams * times
    cam_dev, frames, height, width, chans = whole_now.shape
    piece = chans // count
    chunks = whole_now.reshape(cam_dev, frames, height, width, count, piece)
    chunks = jnp.moveaxis(chunks, 4, 0)
    mine = lax.all_to_all(chunks, axes, 0, 0, tiled=True)
    mine = mine.reshape(cams, times, cam_dev, frames, height, width, piece)
    tail = mine[:, : times - 1, :, frames - (KT - 1) :]
    head = jnp.zeros((cams, 1) + tail.shape[2:], mine.dtype)
    before = jnp.concatenate([head, tail], axis=1)
    timed_all = jnp.concatenate([before, mine], axis=3)
    timed_all = timed_all.reshape(count, cam_dev, frames + KT - 1, height, width, piece)
    specs = ("CDHWN", "IDHWO", "DHWNC")
    first = lax.all_gather(dpre5[:1], axes, axis=0, tiled=True)
    rest = gathered(gathered(dpre5[1:], "tm"), "cam")
    rest = rest.reshape(count, cam_dev - 1, *dpre5.shape[1:])
    rest = rest.reshape(count * (cam_dev - 1), *dpre5.shape[1:])
    timed_rest = timed_all[:, 1:].reshape(count * (cam_dev - 1), *timed_all.shape[2:])
    part = conv3d(timed_all[:, 0], first, space_pad, specs)
    part = part + conv3d(timed_rest, rest, space_pad, specs)
    part = part.astype(jnp.bfloat16)
    return lax.all_gather(part, axes, axis=3, tiled=True)


def joining_matrix(rig_sizes, camera_order, owner_slot):
    robots = rig_sizes.shape[0]
    ends = jnp.cumsum(rig_sizes)
    robot_of = jnp.sum((ends[None, :] <= camera_order[:, None]).astype(jnp.int32), axis=1)
    member = robot_of[:, None] == jnp.arange(robots, dtype=jnp.int32)[None, :]
    slot_of = jnp.sum(jnp.where(member, owner_slot[None, :], 0), axis=1)
    count_of = jnp.sum(jnp.where(member, rig_sizes[None, :], 0), axis=1)
    share = 1.0 / count_of.astype(jnp.float32)
    placed = slot_of[None, :] == jnp.arange(robots, dtype=jnp.int32)[:, None]
    return jnp.where(placed, share[None, :], jnp.zeros_like(share)[None, :])


def body(video, conv_weight, proj_weight, rig_sizes, camera_order, owner_slot, cotangent):
    cam_dev, frames, height, width, half_chan = video.shape
    pad_half = KS // 2
    lat_width = proj_weight.shape[1]
    out_half = conv_weight.shape[2]
    whole_now = lax.all_gather(video, "chan", axis=4, tiled=True)
    whole_cache = shifted(whole_now[:, frames - (KT - 1) :], "tm", 1)
    timed = jnp.concatenate([whole_cache, whole_now], axis=1)
    kernel = conv_weight.reshape(KT, KS, KS, conv_weight.shape[1], out_half)
    space_pad = [(0, 0), (pad_half, pad_half), (pad_half, pad_half)]
    pre5 = conv3d(timed, kernel, space_pad, ("NDHWC", "DHWIO", "NDHWC"))
    pre = pre5.reshape(-1, out_half)
    sigma = jax.nn.sigmoid(pre)
    act = (pre * sigma).astype(jnp.bfloat16)
    latent_part = jnp.dot(act, proj_weight, preferred_element_type=jnp.float32)
    latent = lax.psum(latent_part, "chan").astype(jnp.bfloat16)
    mixing = joining_matrix(rig_sizes, camera_order, owner_slot)
    cam_index = lax.axis_index("cam")
    my_row = lax.dynamic_slice_in_dim(mixing, cam_index, 1, 0)
    latent_maps = latent.reshape(cam_dev, frames, height, width * lat_width)
    block_in = gathered(latent_maps, "cam")
    flat_in = block_in.reshape(block_in.shape[0], -1).astype(jnp.float32)
    added = jnp.dot(
        my_row, flat_in, precision=lax.Precision.HIGHEST, preferred_element_type=jnp.float32
    )
    robot_latent = added.reshape(1, frames, height, width * lat_width)
    my_cols = lax.dynamic_slice_in_dim(mixing, cam_index * cam_dev, cam_dev, 1)
    block_in = gathered(cotangent, "cam")
    flat_in = block_in.reshape(block_in.shape[0], -1).astype(jnp.float32)
    spread = lax.dot_general(
        my_cols,
        flat_in,
        (((0,), (0,)), ((), ())),
        precision=lax.Precision.HIGHEST,
        preferred_element_type=jnp.float32,
    )
    dlatent = spread.astype(jnp.bfloat16).reshape(-1, lat_width)
    grad_proj_local = lax.dot_general(
        act, dlatent, (((0,), (0,)), ((), ())), preferred_element_type=jnp.float32
    )
    dact = lax.dot_general(
        dlatent, proj_weight, (((1,), (1,)), ((), ())), preferred_element_type=jnp.float32
    )
    dpre = (dact * sigma * (1.0 + pre * (1.0 - sigma))).astype(jnp.bfloat16)
    dpre5 = dpre.reshape(cam_dev, frames, height, width, out_half)
    if lax.axis_size("cam") * lax.axis_size("tm") <= 8:
        grad_conv = weight_grad_sliced(whole_now, dpre5, space_pad).reshape(
            KT * KS * KS, -1, out_half
        )
    else:
        grad_conv_local = conv3d(timed, dpre5, space_pad, ("CDHWN", "IDHWO", "DHWNC"))
        grad_conv_local = grad_conv_local.reshape(KT * KS * KS, -1, out_half)
        grad_conv_part = lax.psum_scatter(
            grad_conv_local, ("cam", "tm"), scatter_dimension=1, tiled=True
        )
        grad_conv = lax.all_gather(
            grad_conv_part.astype(jnp.bfloat16), ("cam", "tm"), axis=1, tiled=True
        )
    grad_proj = jnp.sum(gathered(gathered(grad_proj_local[None], "tm"), "cam"), axis=0)
    flipped = kernel[::-1, ::-1, ::-1]
    back_specs = ("NDHWC", "DHWOI", "NDHWC")
    head_pad = [(KT - 1, 0), (pad_half, pad_half), (pad_half, pad_half)]
    cache_part = conv3d(dpre5[:, : KT - 1], flipped, head_pad, back_specs)
    incoming = shifted(cache_part, "tm", -1)
    tail_pad = [(0, KT - 1), (pad_half, pad_half), (pad_half, pad_half)]
    own_part = conv3d(dpre5, flipped, tail_pad, back_specs)
    own_part = own_part.at[:, frames - (KT - 1) :].add(incoming)
    rounded = own_part.astype(jnp.bfloat16)
    chan_count = lax.axis_size("chan")
    chan_index = lax.axis_index("chan")
    width_out = rounded.shape[4] // chan_count
    summed = lax.dynamic_slice_in_dim(rounded, chan_index * width_out, width_out, 4).astype(
        jnp.float32
    )
    for step in range(1, chan_count):
        target = (chan_index + step) % chan_count
        sent = lax.dynamic_slice_in_dim(rounded, target * width_out, width_out, 4)
        pairs = [(i, (i + step) % chan_count) for i in range(chan_count)]
        summed = summed + lax.ppermute(sent, "chan", pairs).astype(jnp.float32)
    grad_video = summed.astype(jnp.bfloat16)
    return (robot_latent, grad_conv, grad_proj, grad_video)


def solution(mesh):
    return jax.shard_map(
        body,
        mesh=mesh,
        in_specs=(
            P(("groups", "cam"), "tm", None, None, "chan"),
            P(None, None, "chan"),
            P("chan", None),
            P("groups"),
            P("groups"),
            P("groups"),
            P(("groups", "cam"), "tm", None, None),
        ),
        out_specs=(
            P(("groups", "cam"), "tm", None, None),
            P("groups", None, "chan"),
            P(("groups", "chan"), None),
            P(("groups", "cam"), "tm", None, None, "chan"),
        ),
        check_vma=False,
    )
```

```python
import jax
import jax.numpy as jnp
from jax import lax
from jax.sharding import PartitionSpec as P

KT = 3
KS = 3


def shifted(shard, axis, by):
    size = lax.axis_size(axis)
    pairs = [(i, i + by) for i in range(size) if 0 <= i + by < size]
    return lax.ppermute(shard, axis, pairs)


def gathered(block, axis):
    size = lax.axis_size(axis)
    if size & (size - 1):
        return lax.all_gather(block, axis, axis=0, tiled=True)
    index = lax.axis_index(axis)
    blocks = block
    step = 1
    while step < size:
        pairs = [(i, i ^ step) for i in range(size)]
        other = lax.ppermute(blocks, axis, pairs)
        upper = (index & step) != 0
        blocks = jnp.where(
            upper,
            jnp.concatenate([other, blocks], axis=0),
            jnp.concatenate([blocks, other], axis=0),
        )
        step *= 2
    return blocks


def conv3d(lhs, rhs, padding, specs):
    return lax.conv_general_dilated(
        lhs,
        rhs,
        window_strides=(1, 1, 1),
        padding=padding,
        dimension_numbers=specs,
        preferred_element_type=jnp.float32,
    )


def weight_grad_sliced(timed, dpre5, space_pad):
    axes = ("cam", "tm")
    mine = lax.all_to_all(timed, axes, 4, 0, tiled=True)
    dpre_all = lax.all_gather(dpre5, axes, axis=0, tiled=True)
    part = conv3d(mine, dpre_all, space_pad, ("CDHWN", "IDHWO", "DHWNC"))
    part = part.astype(jnp.bfloat16)
    return lax.all_gather(part, axes, axis=3, tiled=True)

def joining_matrix(rig_sizes, camera_order, owner_slot):
    robots = rig_sizes.shape[0]
    ends = jnp.cumsum(rig_sizes)
    robot_of = jnp.sum((ends[None, :] <= camera_order[:, None]).astype(jnp.int32), axis=1)
    member = robot_of[:, None] == jnp.arange(robots, dtype=jnp.int32)[None, :]
    slot_of = jnp.sum(jnp.where(member, owner_slot[None, :], 0), axis=1)
    count_of = jnp.sum(jnp.where(member, rig_sizes[None, :], 0), axis=1)
    share = 1.0 / count_of.astype(jnp.float32)
    placed = slot_of[None, :] == jnp.arange(robots, dtype=jnp.int32)[:, None]
    return jnp.where(placed, share[None, :], jnp.zeros_like(share)[None, :])


def body(video, conv_weight, proj_weight, rig_sizes, camera_order, owner_slot, cotangent):
    cam_dev, frames, height, width, half_chan = video.shape
    pad_half = KS // 2
    lat_width = proj_weight.shape[1]
    out_half = conv_weight.shape[2]
    whole_now = lax.all_gather(video, "chan", axis=4, tiled=True)
    whole_cache = shifted(whole_now[:, frames - (KT - 1) :], "tm", 1)
    timed = jnp.concatenate([whole_cache, whole_now], axis=1)
    kernel = conv_weight.reshape(KT, KS, KS, conv_weight.shape[1], out_half)
    space_pad = [(0, 0), (pad_half, pad_half), (pad_half, pad_half)]
    pre5 = conv3d(timed, kernel, space_pad, ("NDHWC", "DHWIO", "NDHWC"))
    pre = pre5.reshape(-1, out_half)
    sigma = jax.nn.sigmoid(pre)
    act = (pre * sigma).astype(jnp.bfloat16)
    latent_part = jnp.dot(act, proj_weight, preferred_element_type=jnp.float32)
    latent = lax.psum(latent_part, "chan").astype(jnp.bfloat16)
    mixing = joining_matrix(rig_sizes, camera_order, owner_slot)
    cam_index = lax.axis_index("cam")
    my_row = lax.dynamic_slice_in_dim(mixing, cam_index, 1, 0)
    latent_maps = latent.reshape(cam_dev, frames, height, width * lat_width)
    block_in = gathered(latent_maps, "cam")
    flat_in = block_in.reshape(block_in.shape[0], -1).astype(jnp.float32)
    added = jnp.dot(
        my_row, flat_in, precision=lax.Precision.HIGHEST, preferred_element_type=jnp.float32
    )
    robot_latent = added.reshape(1, frames, height, width * lat_width)
    my_cols = lax.dynamic_slice_in_dim(mixing, cam_index * cam_dev, cam_dev, 1)
    block_in = gathered(cotangent, "cam")
    flat_in = block_in.reshape(block_in.shape[0], -1).astype(jnp.float32)
    spread = lax.dot_general(
        my_cols,
        flat_in,
        (((0,), (0,)), ((), ())),
        precision=lax.Precision.HIGHEST,
        preferred_element_type=jnp.float32,
    )
    dlatent = spread.astype(jnp.bfloat16).reshape(-1, lat_width)
    grad_proj_local = lax.dot_general(
        act, dlatent, (((0,), (0,)), ((), ())), preferred_element_type=jnp.float32
    )
    dact = lax.dot_general(
        dlatent, proj_weight, (((1,), (1,)), ((), ())), preferred_element_type=jnp.float32
    )
    dpre = (dact * sigma * (1.0 + pre * (1.0 - sigma))).astype(jnp.bfloat16)
    dpre5 = dpre.reshape(cam_dev, frames, height, width, out_half)
    if lax.axis_size("cam") * lax.axis_size("tm") <= 8:
        grad_conv = weight_grad_sliced(timed, dpre5, space_pad).reshape(
            KT * KS * KS, -1, out_half
        )
    else:
        grad_conv_local = conv3d(timed, dpre5, space_pad, ("CDHWN", "IDHWO", "DHWNC"))
        grad_conv_local = grad_conv_local.reshape(KT * KS * KS, -1, out_half)
        grad_conv_part = lax.psum_scatter(
            grad_conv_local, ("cam", "tm"), scatter_dimension=1, tiled=True
        )
        grad_conv = lax.all_gather(
            grad_conv_part.astype(jnp.bfloat16), ("cam", "tm"), axis=1, tiled=True
        )
    grad_proj = jnp.sum(gathered(gathered(grad_proj_local[None], "tm"), "cam"), axis=0)
    flipped = kernel[::-1, ::-1, ::-1]
    back_pad = [(KT - 1, KT - 1), (pad_half, pad_half), (pad_half, pad_half)]
    full_back = conv3d(dpre5, flipped, back_pad, ("NDHWC", "DHWOI", "NDHWC"))
    incoming = shifted(full_back[:, : KT - 1], "tm", -1)
    own_part = full_back[:, KT - 1 :]
    own_part = own_part.at[:, frames - (KT - 1) :].add(incoming)
    rounded = own_part.astype(jnp.bfloat16)
    chan_count = lax.axis_size("chan")
    chan_index = lax.axis_index("chan")
    width_out = rounded.shape[4] // chan_count
    summed = lax.dynamic_slice_in_dim(rounded, chan_index * width_out, width_out, 4).astype(
        jnp.float32
    )
    for step in range(1, chan_count):
        target = (chan_index + step) % chan_count
        sent = lax.dynamic_slice_in_dim(rounded, target * width_out, width_out, 4)
        pairs = [(i, (i + step) % chan_count) for i in range(chan_count)]
        summed = summed + lax.ppermute(sent, "chan", pairs).astype(jnp.float32)
    grad_video = summed.astype(jnp.bfloat16)
    return (robot_latent, grad_conv, grad_proj, grad_video)


def solution(mesh):
    return jax.shard_map(
        body,
        mesh=mesh,
        in_specs=(
            P(("groups", "cam"), "tm", None, None, "chan"),
            P(None, None, "chan"),
            P("chan", None),
            P("groups"),
            P("groups"),
            P("groups"),
            P(("groups", "cam"), "tm", None, None),
        ),
        out_specs=(
            P(("groups", "cam"), "tm", None, None),
            P("groups", None, "chan"),
            P(("groups", "chan"), None),
            P(("groups", "cam"), "tm", None, None, "chan"),
        ),
        check_vma=False,
    )
```

```python
import jax
import jax.numpy as jnp
from jax import lax
from jax.sharding import PartitionSpec as P

KT = 3
KS = 3


def shifted(shard, axis, by):
    size = lax.axis_size(axis)
    pairs = [(i, i + by) for i in range(size) if 0 <= i + by < size]
    return lax.ppermute(shard, axis, pairs)


def gathered(block, axis):
    size = lax.axis_size(axis)
    if size & (size - 1):
        return lax.all_gather(block, axis, axis=0, tiled=True)
    index = lax.axis_index(axis)
    blocks = block
    step = 1
    while step < size:
        pairs = [(i, i ^ step) for i in range(size)]
        other = lax.ppermute(blocks, axis, pairs)
        upper = (index & step) != 0
        blocks = jnp.where(
            upper,
            jnp.concatenate([other, blocks], axis=0),
            jnp.concatenate([blocks, other], axis=0),
        )
        step *= 2
    return blocks


def conv3d(lhs, rhs, padding, specs):
    return lax.conv_general_dilated(
        lhs,
        rhs,
        window_strides=(1, 1, 1),
        padding=padding,
        dimension_numbers=specs,
        preferred_element_type=jnp.float32,
    )


def weight_grad_sliced(whole_now, dpre5, space_pad):
    axes = ("cam", "tm")
    cams = lax.axis_size("cam")
    times = lax.axis_size("tm")
    count = cams * times
    cam_dev, frames, height, width, chans = whole_now.shape
    piece = chans // count
    chunks = whole_now.reshape(cam_dev, frames, height, width, count, piece)
    chunks = jnp.moveaxis(chunks, 4, 0)
    mine = lax.all_to_all(chunks, axes, 0, 0, tiled=True)
    mine = mine.reshape(cams, times, cam_dev, frames, height, width, piece)
    tail = mine[:, : times - 1, :, frames - (KT - 1) :]
    head = jnp.zeros((cams, 1) + tail.shape[2:], mine.dtype)
    before = jnp.concatenate([head, tail], axis=1)
    timed_all = jnp.concatenate([before, mine], axis=3)
    timed_all = timed_all.reshape(count * cam_dev, frames + KT - 1, height, width, piece)
    dpre_all = lax.all_gather(dpre5, axes, axis=0, tiled=True)
    part = conv3d(timed_all, dpre_all, space_pad, ("CDHWN", "IDHWO", "DHWNC"))
    part = part.astype(jnp.bfloat16)
    return lax.all_gather(part, axes, axis=3, tiled=True)


def joining_matrix(rig_sizes, camera_order, owner_slot):
    robots = rig_sizes.shape[0]
    ends = jnp.cumsum(rig_sizes)
    robot_of = jnp.sum((ends[None, :] <= camera_order[:, None]).astype(jnp.int32), axis=1)
    member = robot_of[:, None] == jnp.arange(robots, dtype=jnp.int32)[None, :]
    slot_of = jnp.sum(jnp.where(member, owner_slot[None, :], 0), axis=1)
    count_of = jnp.sum(jnp.where(member, rig_sizes[None, :], 0), axis=1)
    share = 1.0 / count_of.astype(jnp.float32)
    placed = slot_of[None, :] == jnp.arange(robots, dtype=jnp.int32)[:, None]
    return jnp.where(placed, share[None, :], jnp.zeros_like(share)[None, :])


def body(video, conv_weight, proj_weight, rig_sizes, camera_order, owner_slot, cotangent):
    cam_dev, frames, height, width, half_chan = video.shape
    pad_half = KS // 2
    lat_width = proj_weight.shape[1]
    out_half = conv_weight.shape[2]
    whole_now = lax.all_gather(video, "chan", axis=4, tiled=True)
    whole_cache = shifted(whole_now[:, frames - (KT - 1) :], "tm", 1)
    timed = jnp.concatenate([whole_cache, whole_now], axis=1)
    kernel = conv_weight.reshape(KT, KS, KS, conv_weight.shape[1], out_half)
    space_pad = [(0, 0), (pad_half, pad_half), (pad_half, pad_half)]
    pre5 = conv3d(timed, kernel, space_pad, ("NDHWC", "DHWIO", "NDHWC"))
    pre = pre5.reshape(-1, out_half)
    sigma = jax.nn.sigmoid(pre)
    act = (pre * sigma).astype(jnp.bfloat16)
    latent_part = jnp.dot(act, proj_weight, preferred_element_type=jnp.float32)
    latent = lax.psum(latent_part, "chan").astype(jnp.bfloat16)
    mixing = joining_matrix(rig_sizes, camera_order, owner_slot)
    cam_index = lax.axis_index("cam")
    my_row = lax.dynamic_slice_in_dim(mixing, cam_index, 1, 0)
    latent_maps = latent.reshape(cam_dev, frames, height, width * lat_width)
    block_in = gathered(latent_maps, "cam")
    flat_in = block_in.reshape(block_in.shape[0], -1).astype(jnp.float32)
    added = jnp.dot(
        my_row, flat_in, precision=lax.Precision.HIGHEST, preferred_element_type=jnp.float32
    )
    robot_latent = added.reshape(1, frames, height, width * lat_width)
    my_cols = lax.dynamic_slice_in_dim(mixing, cam_index * cam_dev, cam_dev, 1)
    block_in = gathered(cotangent, "cam")
    flat_in = block_in.reshape(block_in.shape[0], -1).astype(jnp.float32)
    spread = lax.dot_general(
        my_cols,
        flat_in,
        (((0,), (0,)), ((), ())),
        precision=lax.Precision.HIGHEST,
        preferred_element_type=jnp.float32,
    )
    dlatent = spread.astype(jnp.bfloat16).reshape(-1, lat_width)
    grad_proj_local = lax.dot_general(
        act, dlatent, (((0,), (0,)), ((), ())), preferred_element_type=jnp.float32
    )
    dact = lax.dot_general(
        dlatent, proj_weight, (((1,), (1,)), ((), ())), preferred_element_type=jnp.float32
    )
    dpre = (dact * sigma * (1.0 + pre * (1.0 - sigma))).astype(jnp.bfloat16)
    dpre5 = dpre.reshape(cam_dev, frames, height, width, out_half)
    if lax.axis_size("cam") * lax.axis_size("tm") <= 8:
        grad_conv = weight_grad_sliced(whole_now, dpre5, space_pad).reshape(
            KT * KS * KS, -1, out_half
        )
    else:
        grad_conv_local = conv3d(timed, dpre5, space_pad, ("CDHWN", "IDHWO", "DHWNC"))
        grad_conv_local = grad_conv_local.reshape(KT * KS * KS, -1, out_half)
        grad_conv_part = lax.psum_scatter(
            grad_conv_local, ("cam", "tm"), scatter_dimension=1, tiled=True
        )
        grad_conv = lax.all_gather(
            grad_conv_part.astype(jnp.bfloat16), ("cam", "tm"), axis=1, tiled=True
        )
    grad_proj = jnp.sum(gathered(gathered(grad_proj_local[None], "tm"), "cam"), axis=0)
    flipped = kernel[::-1, ::-1, ::-1]
    back_pad = [(KT - 1, KT - 1), (pad_half, pad_half), (pad_half, pad_half)]
    full_back = conv3d(dpre5, flipped, back_pad, ("NDHWC", "DHWOI", "NDHWC"))
    incoming = shifted(full_back[:, : KT - 1], "tm", -1)
    own_part = full_back[:, KT - 1 :]
    own_part = own_part.at[:, frames - (KT - 1) :].add(incoming)
    rounded = own_part.astype(jnp.bfloat16)
    chan_count = lax.axis_size("chan")
    chan_index = lax.axis_index("chan")
    width_out = rounded.shape[4] // chan_count
    summed = lax.dynamic_slice_in_dim(rounded, chan_index * width_out, width_out, 4).astype(
        jnp.float32
    )
    for step in range(1, chan_count):
        target = (chan_index + step) % chan_count
        sent = lax.dynamic_slice_in_dim(rounded, target * width_out, width_out, 4)
        pairs = [(i, (i + step) % chan_count) for i in range(chan_count)]
        summed = summed + lax.ppermute(sent, "chan", pairs).astype(jnp.float32)
    grad_video = summed.astype(jnp.bfloat16)
    return (robot_latent, grad_conv, grad_proj, grad_video)


def solution(mesh):
    return jax.shard_map(
        body,
        mesh=mesh,
        in_specs=(
            P(("groups", "cam"), "tm", None, None, "chan"),
            P(None, None, "chan"),
            P("chan", None),
            P("groups"),
            P("groups"),
            P("groups"),
            P(("groups", "cam"), "tm", None, None),
        ),
        out_specs=(
            P(("groups", "cam"), "tm", None, None),
            P("groups", None, "chan"),
            P(("groups", "chan"), None),
            P(("groups", "cam"), "tm", None, None, "chan"),
        ),
        check_vma=False,
    )
```

```python
import jax
import jax.numpy as jnp
from jax import lax
from jax.sharding import PartitionSpec as P

KT = 3
KS = 3


def shifted(shard, axis, by):
    size = lax.axis_size(axis)
    pairs = [(i, i + by) for i in range(size) if 0 <= i + by < size]
    return lax.ppermute(shard, axis, pairs)


def gathered(block, axis):
    size = lax.axis_size(axis)
    if size & (size - 1):
        return lax.all_gather(block, axis, axis=0, tiled=True)
    index = lax.axis_index(axis)
    blocks = block
    step = 1
    while step < size:
        pairs = [(i, i ^ step) for i in range(size)]
        other = lax.ppermute(blocks, axis, pairs)
        upper = (index & step) != 0
        blocks = jnp.where(
            upper,
            jnp.concatenate([other, blocks], axis=0),
            jnp.concatenate([blocks, other], axis=0),
        )
        step *= 2
    return blocks


def conv3d(lhs, rhs, padding, specs):
    return lax.conv_general_dilated(
        lhs,
        rhs,
        window_strides=(1, 1, 1),
        padding=padding,
        dimension_numbers=specs,
        preferred_element_type=jnp.float32,
    )


def weight_grad_sliced(whole_now, dpre5, space_pad):
    axes = ("cam", "tm")
    cams = lax.axis_size("cam")
    times = lax.axis_size("tm")
    count = cams * times
    cam_dev, frames, height, width, chans = whole_now.shape
    piece = chans // count
    chunks = whole_now.reshape(cam_dev, frames, height, width, count, piece)
    chunks = jnp.moveaxis(chunks, 4, 0)
    mine = lax.all_to_all(chunks, axes, 0, 0, tiled=True)
    mine = mine.reshape(cams, times, cam_dev, frames, height, width, piece)
    tail = mine[:, : times - 1, :, frames - (KT - 1) :]
    head = jnp.zeros((cams, 1) + tail.shape[2:], mine.dtype)
    before = jnp.concatenate([head, tail], axis=1)
    timed_all = jnp.concatenate([before, mine], axis=3)
    timed_all = timed_all.reshape(count * cam_dev, frames + KT - 1, height, width, piece)
    dpre_all = lax.all_gather(dpre5, axes, axis=0, tiled=True)
    part = conv3d(timed_all, dpre_all, space_pad, ("CDHWN", "IDHWO", "DHWNC"))
    part = part.astype(jnp.bfloat16)
    return lax.all_gather(part, axes, axis=3, tiled=True)


def xor_gathered(block, axis):
    size = lax.axis_size(axis)
    if size & (size - 1):
        return lax.all_gather(block, axis, axis=0, tiled=True), jnp.arange(size)
    blocks = block
    step = 1
    while step < size:
        pairs = [(i, i ^ step) for i in range(size)]
        blocks = jnp.concatenate([blocks, lax.ppermute(blocks, axis, pairs)], axis=0)
        step *= 2
    return blocks, lax.axis_index(axis) ^ jnp.arange(size)


def joining_matrix(rig_sizes, camera_order, owner_slot):
    robots = rig_sizes.shape[0]
    ends = jnp.cumsum(rig_sizes)
    robot_of = jnp.sum((ends[None, :] <= camera_order[:, None]).astype(jnp.int32), axis=1)
    member = robot_of[:, None] == jnp.arange(robots, dtype=jnp.int32)[None, :]
    slot_of = jnp.sum(jnp.where(member, owner_slot[None, :], 0), axis=1)
    count_of = jnp.sum(jnp.where(member, rig_sizes[None, :], 0), axis=1)
    share = 1.0 / count_of.astype(jnp.float32)
    placed = slot_of[None, :] == jnp.arange(robots, dtype=jnp.int32)[:, None]
    return jnp.where(placed, share[None, :], jnp.zeros_like(share)[None, :])


def body(video, conv_weight, proj_weight, rig_sizes, camera_order, owner_slot, cotangent):
    cam_dev, frames, height, width, half_chan = video.shape
    pad_half = KS // 2
    lat_width = proj_weight.shape[1]
    out_half = conv_weight.shape[2]
    whole_now = lax.all_gather(video, "chan", axis=4, tiled=True)
    whole_cache = shifted(whole_now[:, frames - (KT - 1) :], "tm", 1)
    timed = jnp.concatenate([whole_cache, whole_now], axis=1)
    kernel = conv_weight.reshape(KT, KS, KS, conv_weight.shape[1], out_half)
    space_pad = [(0, 0), (pad_half, pad_half), (pad_half, pad_half)]
    pre5 = conv3d(timed, kernel, space_pad, ("NDHWC", "DHWIO", "NDHWC"))
    pre = pre5.reshape(-1, out_half)
    sigma = jax.nn.sigmoid(pre)
    act = (pre * sigma).astype(jnp.bfloat16)
    latent_part = jnp.dot(act, proj_weight, preferred_element_type=jnp.float32)
    latent = lax.psum(latent_part, "chan").astype(jnp.bfloat16)
    mixing = joining_matrix(rig_sizes, camera_order, owner_slot)
    cam_index = lax.axis_index("cam")
    my_row = lax.dynamic_slice_in_dim(mixing, cam_index, 1, 0)
    latent_maps = latent.reshape(cam_dev, frames, height, width * lat_width)
    block_in, source = xor_gathered(latent_maps, "cam")
    flat_in = block_in.reshape(block_in.shape[0], -1).astype(jnp.float32)
    places = (source[:, None] * cam_dev + jnp.arange(cam_dev)[None, :]).reshape(-1)
    added = jnp.dot(
        my_row[:, places],
        flat_in,
        precision=lax.Precision.HIGHEST,
        preferred_element_type=jnp.float32,
    )
    robot_latent = added.reshape(1, frames, height, width * lat_width)
    my_cols = lax.dynamic_slice_in_dim(mixing, cam_index * cam_dev, cam_dev, 1)
    block_in, source = xor_gathered(cotangent, "cam")
    flat_in = block_in.reshape(block_in.shape[0], -1).astype(jnp.float32)
    rows_per = cotangent.shape[0]
    places = (source[:, None] * rows_per + jnp.arange(rows_per)[None, :]).reshape(-1)
    spread = lax.dot_general(
        my_cols[places],
        flat_in,
        (((0,), (0,)), ((), ())),
        precision=lax.Precision.HIGHEST,
        preferred_element_type=jnp.float32,
    )
    dlatent = spread.astype(jnp.bfloat16).reshape(-1, lat_width)
    grad_proj_local = lax.dot_general(
        act, dlatent, (((0,), (0,)), ((), ())), preferred_element_type=jnp.float32
    )
    dact = lax.dot_general(
        dlatent, proj_weight, (((1,), (1,)), ((), ())), preferred_element_type=jnp.float32
    )
    dpre = (dact * sigma * (1.0 + pre * (1.0 - sigma))).astype(jnp.bfloat16)
    dpre5 = dpre.reshape(cam_dev, frames, height, width, out_half)
    if lax.axis_size("cam") * lax.axis_size("tm") <= 8:
        grad_conv = weight_grad_sliced(whole_now, dpre5, space_pad).reshape(
            KT * KS * KS, -1, out_half
        )
    else:
        grad_conv_local = conv3d(timed, dpre5, space_pad, ("CDHWN", "IDHWO", "DHWNC"))
        grad_conv_local = grad_conv_local.reshape(KT * KS * KS, -1, out_half)
        grad_conv_part = lax.psum_scatter(
            grad_conv_local, ("cam", "tm"), scatter_dimension=1, tiled=True
        )
        grad_conv = lax.all_gather(
            grad_conv_part.astype(jnp.bfloat16), ("cam", "tm"), axis=1, tiled=True
        )
    grad_proj = jnp.sum(gathered(gathered(grad_proj_local[None], "tm"), "cam"), axis=0)
    flipped = kernel[::-1, ::-1, ::-1]
    back_pad = [(KT - 1, KT - 1), (pad_half, pad_half), (pad_half, pad_half)]
    full_back = conv3d(dpre5, flipped, back_pad, ("NDHWC", "DHWOI", "NDHWC"))
    incoming = shifted(full_back[:, : KT - 1], "tm", -1)
    own_part = full_back[:, KT - 1 :]
    own_part = own_part.at[:, frames - (KT - 1) :].add(incoming)
    rounded = own_part.astype(jnp.bfloat16)
    chan_count = lax.axis_size("chan")
    chan_index = lax.axis_index("chan")
    width_out = rounded.shape[4] // chan_count
    summed = lax.dynamic_slice_in_dim(rounded, chan_index * width_out, width_out, 4).astype(
        jnp.float32
    )
    for step in range(1, chan_count):
        target = (chan_index + step) % chan_count
        sent = lax.dynamic_slice_in_dim(rounded, target * width_out, width_out, 4)
        pairs = [(i, (i + step) % chan_count) for i in range(chan_count)]
        summed = summed + lax.ppermute(sent, "chan", pairs).astype(jnp.float32)
    grad_video = summed.astype(jnp.bfloat16)
    return (robot_latent, grad_conv, grad_proj, grad_video)


def solution(mesh):
    return jax.shard_map(
        body,
        mesh=mesh,
        in_specs=(
            P(("groups", "cam"), "tm", None, None, "chan"),
            P(None, None, "chan"),
            P("chan", None),
            P("groups"),
            P("groups"),
            P("groups"),
            P(("groups", "cam"), "tm", None, None),
        ),
        out_specs=(
            P(("groups", "cam"), "tm", None, None),
            P("groups", None, "chan"),
            P(("groups", "chan"), None),
            P(("groups", "cam"), "tm", None, None, "chan"),
        ),
        check_vma=False,
    )
```

```python
import jax
import jax.numpy as jnp
from jax import lax
from jax.sharding import PartitionSpec as P

KT = 3
KS = 3


def shifted(shard, axis, by):
    size = lax.axis_size(axis)
    pairs = [(i, i + by) for i in range(size) if 0 <= i + by < size]
    return lax.ppermute(shard, axis, pairs)


def gathered(block, axis):
    size = lax.axis_size(axis)
    if size & (size - 1):
        return lax.all_gather(block, axis, axis=0, tiled=True)
    index = lax.axis_index(axis)
    blocks = block
    step = 1
    while step < size:
        pairs = [(i, i ^ step) for i in range(size)]
        other = lax.ppermute(blocks, axis, pairs)
        upper = (index & step) != 0
        blocks = jnp.where(
            upper,
            jnp.concatenate([other, blocks], axis=0),
            jnp.concatenate([blocks, other], axis=0),
        )
        step *= 2
    return blocks


def conv3d(lhs, rhs, padding, specs):
    return lax.conv_general_dilated(
        lhs,
        rhs,
        window_strides=(1, 1, 1),
        padding=padding,
        dimension_numbers=specs,
        preferred_element_type=jnp.float32,
    )


def weight_grad_sliced(whole_now, dpre5, space_pad):
    axes = ("cam", "tm")
    cams = lax.axis_size("cam")
    times = lax.axis_size("tm")
    count = cams * times
    cam_dev, frames, height, width, chans = whole_now.shape
    piece = chans // count
    chunks = whole_now.reshape(cam_dev, frames, height, width, count, piece)
    chunks = jnp.moveaxis(chunks, 4, 0)
    mine = lax.all_to_all(chunks, axes, 0, 0, tiled=True)
    mine = mine.reshape(cams, times, cam_dev, frames, height, width, piece)
    tail = mine[:, : times - 1, :, frames - (KT - 1) :]
    head = jnp.zeros((cams, 1) + tail.shape[2:], mine.dtype)
    before = jnp.concatenate([head, tail], axis=1)
    timed_all = jnp.concatenate([before, mine], axis=3)
    timed_all = timed_all.reshape(count * cam_dev, frames + KT - 1, height, width, piece)
    dpre_all = lax.all_gather(dpre5, axes, axis=0, tiled=True)
    part = conv3d(timed_all, dpre_all, space_pad, ("CDHWN", "IDHWO", "DHWNC"))
    part = part.astype(jnp.bfloat16)
    return lax.all_gather(part, axes, axis=3, tiled=True)


def xor_gathered(block, axis):
    size = lax.axis_size(axis)
    if size & (size - 1):
        return lax.all_gather(block, axis, axis=0, tiled=True), jnp.arange(size)
    blocks = block
    step = 1
    while step < size:
        pairs = [(i, i ^ step) for i in range(size)]
        blocks = jnp.concatenate([blocks, lax.ppermute(blocks, axis, pairs)], axis=0)
        step *= 2
    return blocks, lax.axis_index(axis) ^ jnp.arange(size)


def xor_direct(block, axis):
    size = lax.axis_size(axis)
    if size & (size - 1):
        return lax.all_gather(block, axis, axis=0, tiled=True), jnp.arange(size)
    blocks = [block]
    for partner in range(1, size):
        pairs = [(i, i ^ partner) for i in range(size)]
        blocks.append(lax.ppermute(block, axis, pairs))
    return jnp.concatenate(blocks, axis=0), lax.axis_index(axis) ^ jnp.arange(size)


def joining_matrix(rig_sizes, camera_order, owner_slot):
    robots = rig_sizes.shape[0]
    ends = jnp.cumsum(rig_sizes)
    robot_of = jnp.sum((ends[None, :] <= camera_order[:, None]).astype(jnp.int32), axis=1)
    member = robot_of[:, None] == jnp.arange(robots, dtype=jnp.int32)[None, :]
    slot_of = jnp.sum(jnp.where(member, owner_slot[None, :], 0), axis=1)
    count_of = jnp.sum(jnp.where(member, rig_sizes[None, :], 0), axis=1)
    share = 1.0 / count_of.astype(jnp.float32)
    placed = slot_of[None, :] == jnp.arange(robots, dtype=jnp.int32)[:, None]
    return jnp.where(placed, share[None, :], jnp.zeros_like(share)[None, :])


def body(video, conv_weight, proj_weight, rig_sizes, camera_order, owner_slot, cotangent):
    cam_dev, frames, height, width, half_chan = video.shape
    pad_half = KS // 2
    lat_width = proj_weight.shape[1]
    out_half = conv_weight.shape[2]
    whole_now = lax.all_gather(video, "chan", axis=4, tiled=True)
    whole_cache = shifted(whole_now[:, frames - (KT - 1) :], "tm", 1)
    timed = jnp.concatenate([whole_cache, whole_now], axis=1)
    kernel = conv_weight.reshape(KT, KS, KS, conv_weight.shape[1], out_half)
    space_pad = [(0, 0), (pad_half, pad_half), (pad_half, pad_half)]
    pre5 = conv3d(timed, kernel, space_pad, ("NDHWC", "DHWIO", "NDHWC"))
    pre = pre5.reshape(-1, out_half)
    sigma = jax.nn.sigmoid(pre)
    act = (pre * sigma).astype(jnp.bfloat16)
    latent_part = jnp.dot(act, proj_weight, preferred_element_type=jnp.float32)
    latent = lax.psum(latent_part, "chan").astype(jnp.bfloat16)
    mixing = joining_matrix(rig_sizes, camera_order, owner_slot)
    cam_index = lax.axis_index("cam")
    my_row = lax.dynamic_slice_in_dim(mixing, cam_index, 1, 0)
    latent_maps = latent.reshape(cam_dev, frames, height, width * lat_width)
    block_in, source = xor_gathered(latent_maps, "cam")
    flat_in = block_in.reshape(block_in.shape[0], -1).astype(jnp.float32)
    places = (source[:, None] * cam_dev + jnp.arange(cam_dev)[None, :]).reshape(-1)
    added = jnp.dot(
        my_row[:, places],
        flat_in,
        precision=lax.Precision.HIGHEST,
        preferred_element_type=jnp.float32,
    )
    robot_latent = added.reshape(1, frames, height, width * lat_width)
    my_cols = lax.dynamic_slice_in_dim(mixing, cam_index * cam_dev, cam_dev, 1)
    block_in, source = xor_direct(cotangent, "cam")
    flat_in = block_in.reshape(block_in.shape[0], -1).astype(jnp.float32)
    rows_per = cotangent.shape[0]
    places = (source[:, None] * rows_per + jnp.arange(rows_per)[None, :]).reshape(-1)
    spread = lax.dot_general(
        my_cols[places],
        flat_in,
        (((0,), (0,)), ((), ())),
        precision=lax.Precision.HIGHEST,
        preferred_element_type=jnp.float32,
    )
    dlatent = spread.astype(jnp.bfloat16).reshape(-1, lat_width)
    grad_proj_local = lax.dot_general(
        act, dlatent, (((0,), (0,)), ((), ())), preferred_element_type=jnp.float32
    )
    dact = lax.dot_general(
        dlatent, proj_weight, (((1,), (1,)), ((), ())), preferred_element_type=jnp.float32
    )
    dpre = (dact * sigma * (1.0 + pre * (1.0 - sigma))).astype(jnp.bfloat16)
    dpre5 = dpre.reshape(cam_dev, frames, height, width, out_half)
    if lax.axis_size("cam") * lax.axis_size("tm") <= 8:
        grad_conv = weight_grad_sliced(whole_now, dpre5, space_pad).reshape(
            KT * KS * KS, -1, out_half
        )
    else:
        grad_conv_local = conv3d(timed, dpre5, space_pad, ("CDHWN", "IDHWO", "DHWNC"))
        grad_conv_local = grad_conv_local.reshape(KT * KS * KS, -1, out_half)
        grad_conv_part = lax.psum_scatter(
            grad_conv_local, ("cam", "tm"), scatter_dimension=1, tiled=True
        )
        grad_conv = lax.all_gather(
            grad_conv_part.astype(jnp.bfloat16), ("cam", "tm"), axis=1, tiled=True
        )
    grad_proj = jnp.sum(gathered(gathered(grad_proj_local[None], "tm"), "cam"), axis=0)
    flipped = kernel[::-1, ::-1, ::-1]
    back_pad = [(KT - 1, KT - 1), (pad_half, pad_half), (pad_half, pad_half)]
    full_back = conv3d(dpre5, flipped, back_pad, ("NDHWC", "DHWOI", "NDHWC"))
    incoming = shifted(full_back[:, : KT - 1], "tm", -1)
    own_part = full_back[:, KT - 1 :]
    own_part = own_part.at[:, frames - (KT - 1) :].add(incoming)
    rounded = own_part.astype(jnp.bfloat16)
    chan_count = lax.axis_size("chan")
    chan_index = lax.axis_index("chan")
    width_out = rounded.shape[4] // chan_count
    summed = lax.dynamic_slice_in_dim(rounded, chan_index * width_out, width_out, 4).astype(
        jnp.float32
    )
    for step in range(1, chan_count):
        target = (chan_index + step) % chan_count
        sent = lax.dynamic_slice_in_dim(rounded, target * width_out, width_out, 4)
        pairs = [(i, (i + step) % chan_count) for i in range(chan_count)]
        summed = summed + lax.ppermute(sent, "chan", pairs).astype(jnp.float32)
    grad_video = summed.astype(jnp.bfloat16)
    return (robot_latent, grad_conv, grad_proj, grad_video)


def solution(mesh):
    return jax.shard_map(
        body,
        mesh=mesh,
        in_specs=(
            P(("groups", "cam"), "tm", None, None, "chan"),
            P(None, None, "chan"),
            P("chan", None),
            P("groups"),
            P("groups"),
            P("groups"),
            P(("groups", "cam"), "tm", None, None),
        ),
        out_specs=(
            P(("groups", "cam"), "tm", None, None),
            P("groups", None, "chan"),
            P(("groups", "chan"), None),
            P(("groups", "cam"), "tm", None, None, "chan"),
        ),
        check_vma=False,
    )
```

```python
import jax
import jax.numpy as jnp
from jax import lax
from jax.sharding import PartitionSpec as P

KT = 3
KS = 3


def shifted(shard, axis, by):
    size = lax.axis_size(axis)
    pairs = [(i, i + by) for i in range(size) if 0 <= i + by < size]
    return lax.ppermute(shard, axis, pairs)


def gathered(block, axis):
    size = lax.axis_size(axis)
    if size & (size - 1):
        return lax.all_gather(block, axis, axis=0, tiled=True)
    index = lax.axis_index(axis)
    blocks = block
    step = 1
    while step < size:
        pairs = [(i, i ^ step) for i in range(size)]
        other = lax.ppermute(blocks, axis, pairs)
        upper = (index & step) != 0
        blocks = jnp.where(
            upper,
            jnp.concatenate([other, blocks], axis=0),
            jnp.concatenate([blocks, other], axis=0),
        )
        step *= 2
    return blocks


def conv3d(lhs, rhs, padding, specs):
    return lax.conv_general_dilated(
        lhs,
        rhs,
        window_strides=(1, 1, 1),
        padding=padding,
        dimension_numbers=specs,
        preferred_element_type=jnp.float32,
    )


def weight_grad_sliced(whole_now, dpre5, space_pad):
    axes = ("cam", "tm")
    cams = lax.axis_size("cam")
    times = lax.axis_size("tm")
    count = cams * times
    cam_dev, frames, height, width, chans = whole_now.shape
    piece = chans // count
    chunks = whole_now.reshape(cam_dev, frames, height, width, count, piece)
    chunks = jnp.moveaxis(chunks, 4, 0)
    mine = lax.all_to_all(chunks, axes, 0, 0, tiled=True)
    mine = mine.reshape(cams, times, cam_dev, frames, height, width, piece)
    tail = mine[:, : times - 1, :, frames - (KT - 1) :]
    head = jnp.zeros((cams, 1) + tail.shape[2:], mine.dtype)
    before = jnp.concatenate([head, tail], axis=1)
    timed_all = jnp.concatenate([before, mine], axis=3)
    timed_all = timed_all.reshape(count * cam_dev, frames + KT - 1, height, width, piece)
    dpre_all = lax.all_gather(dpre5, axes, axis=0, tiled=True)
    padded_all = jnp.pad(timed_all, ((0, 0), (0, 0)) + tuple(space_pad[1:]) + ((0, 0),))
    swap_pad = [(KT - 1, KT - 1), (KS - 1, KS - 1), (KS - 1, KS - 1)]
    part = conv3d(dpre_all, padded_all, swap_pad, ("CDHWN", "IDHWO", "DHWCN"))
    part = part[::-1, ::-1, ::-1]
    part = part.astype(jnp.bfloat16)
    return lax.all_gather(part, axes, axis=3, tiled=True)


def xor_gathered(block, axis):
    size = lax.axis_size(axis)
    if size & (size - 1):
        return lax.all_gather(block, axis, axis=0, tiled=True), jnp.arange(size)
    blocks = block
    step = 1
    while step < size:
        pairs = [(i, i ^ step) for i in range(size)]
        blocks = jnp.concatenate([blocks, lax.ppermute(blocks, axis, pairs)], axis=0)
        step *= 2
    return blocks, lax.axis_index(axis) ^ jnp.arange(size)


def joining_matrix(rig_sizes, camera_order, owner_slot):
    robots = rig_sizes.shape[0]
    ends = jnp.cumsum(rig_sizes)
    robot_of = jnp.sum((ends[None, :] <= camera_order[:, None]).astype(jnp.int32), axis=1)
    member = robot_of[:, None] == jnp.arange(robots, dtype=jnp.int32)[None, :]
    slot_of = jnp.sum(jnp.where(member, owner_slot[None, :], 0), axis=1)
    count_of = jnp.sum(jnp.where(member, rig_sizes[None, :], 0), axis=1)
    share = 1.0 / count_of.astype(jnp.float32)
    placed = slot_of[None, :] == jnp.arange(robots, dtype=jnp.int32)[:, None]
    return jnp.where(placed, share[None, :], jnp.zeros_like(share)[None, :])


def body(video, conv_weight, proj_weight, rig_sizes, camera_order, owner_slot, cotangent):
    cam_dev, frames, height, width, half_chan = video.shape
    pad_half = KS // 2
    lat_width = proj_weight.shape[1]
    out_half = conv_weight.shape[2]
    whole_now = lax.all_gather(video, "chan", axis=4, tiled=True)
    whole_cache = shifted(whole_now[:, frames - (KT - 1) :], "tm", 1)
    timed = jnp.concatenate([whole_cache, whole_now], axis=1)
    kernel = conv_weight.reshape(KT, KS, KS, conv_weight.shape[1], out_half)
    space_pad = [(0, 0), (pad_half, pad_half), (pad_half, pad_half)]
    pre5 = conv3d(timed, kernel, space_pad, ("NDHWC", "DHWIO", "NDHWC"))
    pre = pre5.reshape(-1, out_half)
    sigma = jax.nn.sigmoid(pre)
    act = (pre * sigma).astype(jnp.bfloat16)
    latent_part = jnp.dot(act, proj_weight, preferred_element_type=jnp.float32)
    latent = lax.psum(latent_part, "chan").astype(jnp.bfloat16)
    mixing = joining_matrix(rig_sizes, camera_order, owner_slot)
    cam_index = lax.axis_index("cam")
    my_row = lax.dynamic_slice_in_dim(mixing, cam_index, 1, 0)
    latent_maps = latent.reshape(cam_dev, frames, height, width * lat_width)
    block_in, source = xor_gathered(latent_maps, "cam")
    flat_in = block_in.reshape(block_in.shape[0], -1).astype(jnp.float32)
    places = (source[:, None] * cam_dev + jnp.arange(cam_dev)[None, :]).reshape(-1)
    added = jnp.dot(
        my_row[:, places],
        flat_in,
        precision=lax.Precision.HIGHEST,
        preferred_element_type=jnp.float32,
    )
    robot_latent = added.reshape(1, frames, height, width * lat_width)
    my_cols = lax.dynamic_slice_in_dim(mixing, cam_index * cam_dev, cam_dev, 1)
    block_in, source = xor_gathered(cotangent, "cam")
    flat_in = block_in.reshape(block_in.shape[0], -1).astype(jnp.float32)
    rows_per = cotangent.shape[0]
    places = (source[:, None] * rows_per + jnp.arange(rows_per)[None, :]).reshape(-1)
    spread = lax.dot_general(
        my_cols[places],
        flat_in,
        (((0,), (0,)), ((), ())),
        precision=lax.Precision.HIGHEST,
        preferred_element_type=jnp.float32,
    )
    dlatent = spread.astype(jnp.bfloat16).reshape(-1, lat_width)
    grad_proj_local = lax.dot_general(
        act, dlatent, (((0,), (0,)), ((), ())), preferred_element_type=jnp.float32
    )
    dact = lax.dot_general(
        dlatent, proj_weight, (((1,), (1,)), ((), ())), preferred_element_type=jnp.float32
    )
    dpre = (dact * sigma * (1.0 + pre * (1.0 - sigma))).astype(jnp.bfloat16)
    dpre5 = dpre.reshape(cam_dev, frames, height, width, out_half)
    if lax.axis_size("cam") * lax.axis_size("tm") <= 8:
        grad_conv = weight_grad_sliced(whole_now, dpre5, space_pad).reshape(
            KT * KS * KS, -1, out_half
        )
    else:
        grad_conv_local = conv3d(timed, dpre5, space_pad, ("CDHWN", "IDHWO", "DHWNC"))
        grad_conv_local = grad_conv_local.reshape(KT * KS * KS, -1, out_half)
        grad_conv_part = lax.psum_scatter(
            grad_conv_local, ("cam", "tm"), scatter_dimension=1, tiled=True
        )
        grad_conv = lax.all_gather(
            grad_conv_part.astype(jnp.bfloat16), ("cam", "tm"), axis=1, tiled=True
        )
    grad_proj = jnp.sum(gathered(gathered(grad_proj_local[None], "tm"), "cam"), axis=0)
    flipped = kernel[::-1, ::-1, ::-1]
    back_pad = [(KT - 1, KT - 1), (pad_half, pad_half), (pad_half, pad_half)]
    full_back = conv3d(dpre5, flipped, back_pad, ("NDHWC", "DHWOI", "NDHWC"))
    incoming = shifted(full_back[:, : KT - 1], "tm", -1)
    own_part = full_back[:, KT - 1 :]
    own_part = own_part.at[:, frames - (KT - 1) :].add(incoming)
    rounded = own_part.astype(jnp.bfloat16)
    chan_count = lax.axis_size("chan")
    chan_index = lax.axis_index("chan")
    width_out = rounded.shape[4] // chan_count
    summed = lax.dynamic_slice_in_dim(rounded, chan_index * width_out, width_out, 4).astype(
        jnp.float32
    )
    for step in range(1, chan_count):
        target = (chan_index + step) % chan_count
        sent = lax.dynamic_slice_in_dim(rounded, target * width_out, width_out, 4)
        pairs = [(i, (i + step) % chan_count) for i in range(chan_count)]
        summed = summed + lax.ppermute(sent, "chan", pairs).astype(jnp.float32)
    grad_video = summed.astype(jnp.bfloat16)
    return (robot_latent, grad_conv, grad_proj, grad_video)


def solution(mesh):
    return jax.shard_map(
        body,
        mesh=mesh,
        in_specs=(
            P(("groups", "cam"), "tm", None, None, "chan"),
            P(None, None, "chan"),
            P("chan", None),
            P("groups"),
            P("groups"),
            P("groups"),
            P(("groups", "cam"), "tm", None, None),
        ),
        out_specs=(
            P(("groups", "cam"), "tm", None, None),
            P("groups", None, "chan"),
            P(("groups", "chan"), None),
            P(("groups", "cam"), "tm", None, None, "chan"),
        ),
        check_vma=False,
    )
```

```python
import jax
import jax.numpy as jnp
from jax import lax
from jax.sharding import PartitionSpec as P

KT = 3
KS = 3


def shifted(shard, axis, by):
    size = lax.axis_size(axis)
    pairs = [(i, i + by) for i in range(size) if 0 <= i + by < size]
    return lax.ppermute(shard, axis, pairs)


def gathered(block, axis):
    size = lax.axis_size(axis)
    if size & (size - 1):
        return lax.all_gather(block, axis, axis=0, tiled=True)
    index = lax.axis_index(axis)
    blocks = block
    step = 1
    while step < size:
        pairs = [(i, i ^ step) for i in range(size)]
        other = lax.ppermute(blocks, axis, pairs)
        upper = (index & step) != 0
        blocks = jnp.where(
            upper,
            jnp.concatenate([other, blocks], axis=0),
            jnp.concatenate([blocks, other], axis=0),
        )
        step *= 2
    return blocks


def conv3d(lhs, rhs, padding, specs):
    return lax.conv_general_dilated(
        lhs,
        rhs,
        window_strides=(1, 1, 1),
        padding=padding,
        dimension_numbers=specs,
        preferred_element_type=jnp.float32,
    )


def weight_grad_sliced(whole_now, dpre5, space_pad):
    axes = ("cam", "tm")
    cams = lax.axis_size("cam")
    times = lax.axis_size("tm")
    count = cams * times
    cam_dev, frames, height, width, chans = whole_now.shape
    piece = chans // count
    chunks = whole_now.reshape(cam_dev, frames, height, width, count, piece)
    chunks = jnp.moveaxis(chunks, 4, 0)
    mine = lax.all_to_all(chunks, axes, 0, 0, tiled=True)
    mine = mine.reshape(cams, times, cam_dev, frames, height, width, piece)
    tail = mine[:, : times - 1, :, frames - (KT - 1) :]
    head = jnp.zeros((cams, 1) + tail.shape[2:], mine.dtype)
    before = jnp.concatenate([head, tail], axis=1)
    timed_all = jnp.concatenate([before, mine], axis=3)
    timed_all = timed_all.reshape(count * cam_dev, frames + KT - 1, height, width, piece)
    dpre_all = lax.all_gather(dpre5, axes, axis=0, tiled=True)
    part = conv3d(timed_all, dpre_all, space_pad, ("CDHWN", "IDHWO", "DHWNC"))
    part = part.astype(jnp.bfloat16)
    return lax.all_gather(part, axes, axis=3, tiled=True)


def xor_gathered(block, axis):
    size = lax.axis_size(axis)
    if size & (size - 1):
        return lax.all_gather(block, axis, axis=0, tiled=True), jnp.arange(size)
    blocks = block
    step = 1
    while step < size:
        pairs = [(i, i ^ step) for i in range(size)]
        blocks = jnp.concatenate([blocks, lax.ppermute(blocks, axis, pairs)], axis=0)
        step *= 2
    return blocks, lax.axis_index(axis) ^ jnp.arange(size)


def joining_matrix(rig_sizes, camera_order, owner_slot):
    robots = rig_sizes.shape[0]
    ends = jnp.cumsum(rig_sizes)
    robot_of = jnp.sum((ends[None, :] <= camera_order[:, None]).astype(jnp.int32), axis=1)
    member = robot_of[:, None] == jnp.arange(robots, dtype=jnp.int32)[None, :]
    slot_of = jnp.sum(jnp.where(member, owner_slot[None, :], 0), axis=1)
    count_of = jnp.sum(jnp.where(member, rig_sizes[None, :], 0), axis=1)
    share = 1.0 / count_of.astype(jnp.float32)
    placed = slot_of[None, :] == jnp.arange(robots, dtype=jnp.int32)[:, None]
    return jnp.where(placed, share[None, :], jnp.zeros_like(share)[None, :])


def body(video, conv_weight, proj_weight, rig_sizes, camera_order, owner_slot, cotangent):
    cam_dev, frames, height, width, half_chan = video.shape
    pad_half = KS // 2
    lat_width = proj_weight.shape[1]
    out_half = conv_weight.shape[2]
    cache_half = shifted(video[:, frames - (KT - 1) :], "tm", 1)
    whole_now = lax.all_gather(video, "chan", axis=4, tiled=True)
    whole_cache = lax.all_gather(cache_half, "chan", axis=4, tiled=True)
    timed = jnp.concatenate([whole_cache, whole_now], axis=1)
    kernel = conv_weight.reshape(KT, KS, KS, conv_weight.shape[1], out_half)
    space_pad = [(0, 0), (pad_half, pad_half), (pad_half, pad_half)]
    pre5 = conv3d(timed, kernel, space_pad, ("NDHWC", "DHWIO", "NDHWC"))
    pre = pre5.reshape(-1, out_half)
    sigma = jax.nn.sigmoid(pre)
    act = (pre * sigma).astype(jnp.bfloat16)
    latent_part = jnp.dot(act, proj_weight, preferred_element_type=jnp.float32)
    latent = lax.psum(latent_part, "chan").astype(jnp.bfloat16)
    mixing = joining_matrix(rig_sizes, camera_order, owner_slot)
    cam_index = lax.axis_index("cam")
    my_row = lax.dynamic_slice_in_dim(mixing, cam_index, 1, 0)
    latent_maps = latent.reshape(cam_dev, frames, height, width * lat_width)
    block_in, source = xor_gathered(latent_maps, "cam")
    flat_in = block_in.reshape(block_in.shape[0], -1).astype(jnp.float32)
    places = (source[:, None] * cam_dev + jnp.arange(cam_dev)[None, :]).reshape(-1)
    added = jnp.dot(
        my_row[:, places],
        flat_in,
        precision=lax.Precision.HIGHEST,
        preferred_element_type=jnp.float32,
    )
    robot_latent = added.reshape(1, frames, height, width * lat_width)
    my_cols = lax.dynamic_slice_in_dim(mixing, cam_index * cam_dev, cam_dev, 1)
    block_in, source = xor_gathered(cotangent, "cam")
    flat_in = block_in.reshape(block_in.shape[0], -1).astype(jnp.float32)
    rows_per = cotangent.shape[0]
    places = (source[:, None] * rows_per + jnp.arange(rows_per)[None, :]).reshape(-1)
    spread = lax.dot_general(
        my_cols[places],
        flat_in,
        (((0,), (0,)), ((), ())),
        precision=lax.Precision.HIGHEST,
        preferred_element_type=jnp.float32,
    )
    dlatent = spread.astype(jnp.bfloat16).reshape(-1, lat_width)
    grad_proj_local = lax.dot_general(
        act, dlatent, (((0,), (0,)), ((), ())), preferred_element_type=jnp.float32
    )
    dact = lax.dot_general(
        dlatent, proj_weight, (((1,), (1,)), ((), ())), preferred_element_type=jnp.float32
    )
    dpre = (dact * sigma * (1.0 + pre * (1.0 - sigma))).astype(jnp.bfloat16)
    dpre5 = dpre.reshape(cam_dev, frames, height, width, out_half)
    if lax.axis_size("cam") * lax.axis_size("tm") <= 8:
        grad_conv = weight_grad_sliced(whole_now, dpre5, space_pad).reshape(
            KT * KS * KS, -1, out_half
        )
    else:
        grad_conv_local = conv3d(timed, dpre5, space_pad, ("CDHWN", "IDHWO", "DHWNC"))
        grad_conv_local = grad_conv_local.reshape(KT * KS * KS, -1, out_half)
        grad_conv_part = lax.psum_scatter(
            grad_conv_local, ("cam", "tm"), scatter_dimension=1, tiled=True
        )
        grad_conv = lax.all_gather(
            grad_conv_part.astype(jnp.bfloat16), ("cam", "tm"), axis=1, tiled=True
        )
    grad_proj = jnp.sum(gathered(gathered(grad_proj_local[None], "tm"), "cam"), axis=0)
    flipped = kernel[::-1, ::-1, ::-1]
    back_pad = [(KT - 1, KT - 1), (pad_half, pad_half), (pad_half, pad_half)]
    full_back = conv3d(dpre5, flipped, back_pad, ("NDHWC", "DHWOI", "NDHWC"))
    incoming = shifted(full_back[:, : KT - 1], "tm", -1)
    own_part = full_back[:, KT - 1 :]
    own_part = own_part.at[:, frames - (KT - 1) :].add(incoming)
    rounded = own_part.astype(jnp.bfloat16)
    chan_count = lax.axis_size("chan")
    chan_index = lax.axis_index("chan")
    width_out = rounded.shape[4] // chan_count
    summed = lax.dynamic_slice_in_dim(rounded, chan_index * width_out, width_out, 4).astype(
        jnp.float32
    )
    for step in range(1, chan_count):
        target = (chan_index + step) % chan_count
        sent = lax.dynamic_slice_in_dim(rounded, target * width_out, width_out, 4)
        pairs = [(i, (i + step) % chan_count) for i in range(chan_count)]
        summed = summed + lax.ppermute(sent, "chan", pairs).astype(jnp.float32)
    grad_video = summed.astype(jnp.bfloat16)
    return (robot_latent, grad_conv, grad_proj, grad_video)


def solution(mesh):
    return jax.shard_map(
        body,
        mesh=mesh,
        in_specs=(
            P(("groups", "cam"), "tm", None, None, "chan"),
            P(None, None, "chan"),
            P("chan", None),
            P("groups"),
            P("groups"),
            P("groups"),
            P(("groups", "cam"), "tm", None, None),
        ),
        out_specs=(
            P(("groups", "cam"), "tm", None, None),
            P("groups", None, "chan"),
            P(("groups", "chan"), None),
            P(("groups", "cam"), "tm", None, None, "chan"),
        ),
        check_vma=False,
    )
```
